128 devices in a mesh: dp: 8 (over z_hi, y), head: 16 (over z_lo, x, core).
Axes of the slice: x: 4, y: 4, z: 4 (z_hi: 2, z_lo: 2; z = z_hi * 2 + z_lo), core: 2. Of those that a mesh axis runs over, the one named last changes fastest.
Arguments:
- queries: bfloat16 [4096, 128, 192], P('dp', 'head'), may hold values from -6 to 6
- latent: bfloat16 [4096, 576], P('dp'), may hold values from -6 to 6
- prefix: bfloat16 [256, 576], replicated, may hold values from -12 to 12
- kv_up: bfloat16 [512, 128, 256], P(None, 'head'), may hold values from -0.25 to 0.25
- out_grad: bfloat16 [4096, 128, 128], P('dp', 'head'), may hold values from -12 to 12
- lengths: int32 [8], P('dp'), may hold values from 64 to 512, as said below
- positions: int32 [8, 512], P('dp'), may hold values from 0 to 4606, as said below
Outputs:
- query_grad: bfloat16 [4096, 128, 192], P('dp', 'head')
- latent_grad: float32 [4096, 576], P(('dp', 'head'))
- up_grad: float32 [512, 128, 256], P('dp', 'head')
- prefix_grad: float32 [256, 576], replicated
The draws below stay inside these ranges and needn't reach their ends.
Inputs may be any that keep to these rules, and one draw needn't show every extreme that they name: Sequence b's valid tokens are its first lengths[b] tokens. Within a sequence the positions rise by one from token to token.
All inputs are finite; a program needn't handle non-finite values.
Results may differ from the reference program's by a relative error of at most 0.018.
Values may be sent and summed in bfloat16 or wider, within the bound.
No kernel may reach another device: no remote copies, remote signals or barrier semaphores. Data moves between devices by JAX's collectives and lax.ppermute only.
A program may use at most 128 MiB of HBM per device.

```python
import jax
import jax.numpy as jnp
from jax import lax

HEADS = 128
NOPE = 128
ROPE = 64
VDIM = 128
LATENT = 512
PREFIX = 256
SEQ = 512
BATCH = 8
TOKENS = 4096


def offsets_for(key):
    drawn = jax.random.randint(jax.random.fold_in(key, 11), (BATCH,), 0, 4096)
    shuffled = jax.random.permutation(jax.random.fold_in(key, 13), BATCH)
    drawn = drawn.at[shuffled[0]].set(0)
    return drawn.at[shuffled[1]].set(4095)


def draw_positions(key, part):
    return (offsets_for(key)[:, None] + jnp.arange(SEQ, dtype=jnp.int32)[None, :]).astype(jnp.int32)


def draw_lengths(key, part):
    drawn = jax.random.randint(jax.random.fold_in(key, 23), (BATCH,), SEQ // 8, SEQ + 1)
    shuffled = jax.random.permutation(jax.random.fold_in(key, 29), BATCH)
    drawn = drawn.at[shuffled[0]].set(SEQ)
    return drawn.at[shuffled[1]].set(SEQ // 8).astype(jnp.int32)


def draw_queries(key, part):
    full_shape = (TOKENS, HEADS, NOPE + ROPE)
    drawn = jax.random.truncated_normal(jax.random.fold_in(key, 1), -6.0, 6.0, full_shape, jnp.float32)
    return drawn.astype(jnp.bfloat16)


def draw_prefix(key, part):
    full_shape = (PREFIX, LATENT + ROPE)
    drawn = jax.random.truncated_normal(jax.random.fold_in(key, 3), -6.0, 6.0, full_shape, jnp.float32)
    return drawn.astype(jnp.bfloat16)


def steps_of(own_key, shape, split, smallest, top_value):
    factor_of = 1.0
    for dim, shards_of in split:
        steps = jax.random.uniform(jax.random.fold_in(jax.random.fold_in(own_key, 6), dim), (shards_of,), jnp.float32, smallest / len(split), top_value / len(split))
        factor_of = factor_of * jnp.repeat(jnp.exp(steps), shape[dim] // shards_of).reshape((-1,) + (1,) * (len(shape) - 1 - dim))
    return factor_of


def centred(key, extent, width, most, cuts=(), kind=jnp.bfloat16):
    entries = width * jax.random.normal(key, extent, jnp.float32)
    if cuts:
        entries = entries * steps_of(key, extent, cuts, -0.22, 0.18)
    return jnp.clip(entries, -most, most).astype(kind)


def setup_inputs(seed: int = 0) -> dict:
    streams_of = jax.random.split(jax.random.key(seed), 8)
    queries = draw_queries(jax.random.fold_in(streams_of[7], 71), 0)
    latent = centred(streams_of[1], (TOKENS, LATENT + ROPE), 1.0, 6.0, ((0, 8),))
    prefix = draw_prefix(jax.random.fold_in(streams_of[7], 71), 0)
    kv_up = centred(streams_of[3], (LATENT, HEADS, NOPE + VDIM), LATENT ** -0.5, 0.25, ((1, 16),))
    out_grad = centred(streams_of[4], (TOKENS, HEADS, VDIM), 2.0, 12.0, ((0, 8), (1, 16)))
    lengths = draw_lengths(jax.random.fold_in(streams_of[7], 71), 0)
    positions = draw_positions(jax.random.fold_in(streams_of[7], 71), 0)
    return dict(queries=queries, latent=latent, prefix=prefix, kv_up=kv_up, out_grad=out_grad, lengths=lengths, positions=positions)


def widen(array_in):
    return array_in.astype(jnp.float32)


def angles_of(positions, rope_dim):
    halfway = rope_dim // 2
    frequency = 10000.0 ** (-(jnp.arange(halfway, dtype=jnp.float32) * 2.0 / rope_dim))
    angles = positions.astype(jnp.float32)[:, None] * frequency[None, :]
    return jnp.cos(angles), jnp.sin(angles)


def rotate(values, cosine, sine):
    halfway = values.shape[-1] // 2
    leading = values[..., :halfway]
    trailing = values[..., halfway:]
    return jnp.concatenate([leading * cosine - trailing * sine, trailing * cosine + leading * sine], axis=-1)


def unrotate(values, cosine, sine):
    halfway = values.shape[-1] // 2
    leading = values[..., :halfway]
    trailing = values[..., halfway:]
    return jnp.concatenate([leading * cosine + trailing * sine, trailing * cosine - leading * sine], axis=-1)


def block_gradients(query_nope, query_rope, key_nope, key_rope, values, cotangent, length, prefix_rows):
    score_scale = (query_nope.shape[-1] + query_rope.shape[-1]) ** -0.5
    scores = (jnp.einsum("qhd,khd->hqk", widen(query_nope), widen(key_nope))
              + jnp.einsum("qhr,kr->hqk", widen(query_rope), widen(key_rope))) * score_scale
    row_index = jnp.arange(query_nope.shape[0])
    col_index = jnp.arange(key_nope.shape[0]) - prefix_rows
    allowed = (col_index[None, :] < 0) | ((col_index[None, :] <= row_index[:, None]) & (col_index[None, :] < length))
    scores = jnp.where(allowed[None], scores, -jnp.inf)
    highest = jnp.max(scores, axis=-1, keepdims=True)
    exponent = jnp.exp(scores - highest)
    probability = exponent / jnp.sum(exponent, axis=-1, keepdims=True)
    weights = probability.astype(jnp.bfloat16)
    output = jnp.einsum("hqk,khv->qhv", widen(weights), widen(values))
    row_delta = jnp.sum(widen(cotangent) * output, axis=-1)
    prob_grad = jnp.einsum("qhv,khv->hqk", widen(cotangent), widen(values))
    score_grad = (probability * (prob_grad - jnp.transpose(row_delta)[:, :, None]) * score_scale).astype(jnp.bfloat16)
    nope_query = jnp.einsum("hqk,khd->qhd", widen(score_grad), widen(key_nope))
    rope_query = jnp.einsum("hqk,kr->qhr", widen(score_grad), widen(key_rope))
    nope_key = jnp.einsum("hqk,qhd->khd", widen(score_grad), widen(query_nope))
    rope_key = jnp.einsum("hqk,qhr->kr", widen(score_grad), widen(query_rope))
    value_grad = jnp.einsum("hqk,qhv->khv", widen(weights), widen(cotangent))
    return nope_query, rope_query, nope_key, rope_key, value_grad


def reference(queries, latent, prefix, kv_up, out_grad, lengths, positions):
    group_size = min(HEADS, 8)
    group_count = HEADS // group_size
    key_total = PREFIX + SEQ
    row_width = LATENT + ROPE
    weight_groups = jnp.transpose(kv_up.reshape(LATENT, group_count, group_size, NOPE + VDIM), (1, 0, 2, 3))

    def one_sequence(carry, inputs):
        up_total, prefix_total = carry
        seq_queries, seq_latent, seq_grad, length, seq_positions = inputs
        cosine, sine = angles_of(seq_positions, ROPE)
        query_nope = seq_queries[:, :, :NOPE]
        query_rope = rotate(widen(seq_queries[:, :, NOPE:]), cosine[:, None], sine[:, None]).astype(jnp.bfloat16)
        token_rope = rotate(widen(seq_latent[:, LATENT:]), cosine, sine).astype(jnp.bfloat16)
        source = jnp.concatenate([prefix, jnp.concatenate([seq_latent[:, :LATENT], token_rope], axis=1)], axis=0)
        source_latent = source[:, :LATENT]
        key_rope = source[:, LATENT:]
        live_rows = jnp.arange(SEQ) < length
        cotangent = jnp.where(live_rows[:, None, None], seq_grad, jnp.zeros_like(seq_grad))
        nope_groups = jnp.transpose(query_nope.reshape(SEQ, group_count, group_size, NOPE), (1, 0, 2, 3))
        rope_groups = jnp.transpose(query_rope.reshape(SEQ, group_count, group_size, ROPE), (1, 0, 2, 3))
        grad_groups = jnp.transpose(cotangent.reshape(SEQ, group_count, group_size, VDIM), (1, 0, 2, 3))

        def one_group(source_total, group_inputs):
            weight_part, nope_part, rope_part, cot_part = group_inputs
            projected = jnp.einsum("kl,lhd->khd", widen(source_latent), widen(weight_part)).astype(jnp.bfloat16)
            nope_query, rope_query, nope_key, rope_key, value_grad = block_gradients(
                nope_part, rope_part, projected[:, :, :NOPE], key_rope, projected[:, :, NOPE:], cot_part, length, PREFIX)
            projected_grad = jnp.concatenate([nope_key, value_grad], axis=-1).astype(jnp.bfloat16)
            up_part = jnp.einsum("kl,khd->lhd", widen(source_latent), widen(projected_grad))
            latent_part = jnp.einsum("khd,lhd->kl", widen(projected_grad), widen(weight_part))
            source_total = source_total + jnp.concatenate([latent_part, rope_key], axis=1)
            query_grad = jnp.concatenate(
                [nope_query, unrotate(rope_query, cosine[:, None], sine[:, None])], axis=-1).astype(jnp.bfloat16)
            return source_total, (query_grad, up_part)

        source_total, (query_groups, up_groups) = lax.scan(
            one_group, jnp.zeros((key_total, row_width), jnp.float32),
            (weight_groups, nope_groups, rope_groups, grad_groups))
        query_grad = jnp.transpose(query_groups, (1, 0, 2, 3)).reshape(SEQ, HEADS, NOPE + ROPE)
        up_seq = jnp.transpose(up_groups, (1, 0, 2, 3)).reshape(LATENT, HEADS, NOPE + VDIM)
        up_round = widen(lax.optimization_barrier(up_seq.astype(jnp.bfloat16)))
        latent_grad = jnp.concatenate(
            [source_total[PREFIX:, :LATENT], unrotate(source_total[PREFIX:, LATENT:], cosine, sine)], axis=1)
        return (up_total + up_round, prefix_total + source_total[:PREFIX]), (query_grad, latent_grad)

    inputs = (queries.reshape(BATCH, SEQ, HEADS, NOPE + ROPE), latent.reshape(BATCH, SEQ, row_width),
              out_grad.reshape(BATCH, SEQ, HEADS, VDIM), lengths, positions)
    start_carry = (jnp.zeros((LATENT, HEADS, NOPE + VDIM), jnp.float32), jnp.zeros((PREFIX, row_width), jnp.float32))
    (up_grad, prefix_grad), (query_grads, latent_grads) = lax.scan(one_sequence, start_carry, inputs)
    return (query_grads.reshape(TOKENS, HEADS, NOPE + ROPE), latent_grads.reshape(TOKENS, row_width),
            up_grad, prefix_grad)
```

```python
import jax
import jax.numpy as jnp
from jax import lax
from jax.sharding import PartitionSpec as P


def angles_of(positions, rope_dim):
    halfway = rope_dim // 2
    frequency = 10000.0 ** (-(jnp.arange(halfway, dtype=jnp.float32) * 2.0 / rope_dim))
    angles = positions.astype(jnp.float32)[:, None] * frequency[None, :]
    return (jnp.cos(angles), jnp.sin(angles))


def rotate(values, cosine, sine):
    halfway = values.shape[-1] // 2
    leading = values[..., :halfway]
    trailing = values[..., halfway:]
    return jnp.concatenate(
        [leading * cosine - trailing * sine, trailing * cosine + leading * sine], axis=-1
    )


def unrotate(values, cosine, sine):
    halfway = values.shape[-1] // 2
    leading = values[..., :halfway]
    trailing = values[..., halfway:]
    return jnp.concatenate(
        [leading * cosine + trailing * sine, trailing * cosine - leading * sine], axis=-1
    )


def block_gradients(
    query_nope, query_rope, key_nope, key_rope, values, cotangent, first_row, length, prefix_rows
):
    score_scale = (query_nope.shape[-1] + query_rope.shape[-1]) ** (-0.5)
    scores = (
        jnp.einsum("qhd,khd->hqk", query_nope, key_nope, preferred_element_type=jnp.float32)
        + jnp.einsum("qhr,kr->hqk", query_rope, key_rope, preferred_element_type=jnp.float32)
    ) * score_scale
    row_index = first_row + jnp.arange(query_nope.shape[0])
    col_index = jnp.arange(key_nope.shape[0]) - prefix_rows
    allowed = (col_index[None, :] < 0) | (col_index[None, :] <= row_index[:, None]) & (
        col_index[None, :] < length
    )
    scores = jnp.where(allowed[None], scores, -jnp.inf)
    highest = jnp.max(scores, axis=-1, keepdims=True)
    exponent = jnp.exp(scores - highest)
    probability = exponent / jnp.sum(exponent, axis=-1, keepdims=True)
    weights = probability.astype(jnp.bfloat16)
    output = jnp.einsum("hqk,khv->qhv", weights, values, preferred_element_type=jnp.float32)
    row_delta = jnp.sum(cotangent.astype(jnp.float32) * output, axis=-1)
    prob_grad = jnp.einsum("qhv,khv->hqk", cotangent, values, preferred_element_type=jnp.float32)
    score_grad = (
        probability * (prob_grad - jnp.transpose(row_delta)[:, :, None]) * score_scale
    ).astype(jnp.bfloat16)
    nope_query = jnp.einsum(
        "hqk,khd->qhd", score_grad, key_nope, preferred_element_type=jnp.float32
    )
    rope_query = jnp.einsum("hqk,kr->qhr", score_grad, key_rope, preferred_element_type=jnp.float32)
    nope_key = jnp.einsum(
        "hqk,qhd->khd", score_grad, query_nope, preferred_element_type=jnp.float32
    )
    rope_key = jnp.einsum("hqk,qhr->kr", score_grad, query_rope, preferred_element_type=jnp.float32)
    value_grad = jnp.einsum("hqk,qhv->khv", weights, cotangent, preferred_element_type=jnp.float32)
    return (nope_query, rope_query, nope_key, rope_key, value_grad)


def on_device(queries, latent, prefix, kv_up, out_grad, lengths, positions):
    seq_len = queries.shape[0]
    latent_dim = kv_up.shape[0]
    value_dim = out_grad.shape[2]
    nope_dim = kv_up.shape[2] - value_dim
    rope_dim = latent.shape[1] - latent_dim
    prefix_rows = prefix.shape[0]
    length = lengths[0]
    cosine, sine = angles_of(positions[0], rope_dim)
    query_nope = queries[:, :, :nope_dim]
    query_rope = rotate(
        queries[:, :, nope_dim:].astype(jnp.float32), cosine[:, None], sine[:, None]
    ).astype(jnp.bfloat16)
    token_rope = rotate(latent[:, latent_dim:].astype(jnp.float32), cosine, sine).astype(
        jnp.bfloat16
    )
    source = jnp.concatenate(
        [prefix, jnp.concatenate([latent[:, :latent_dim], token_rope], axis=1)], axis=0
    )
    source_latent = source[:, :latent_dim]
    key_rope = source[:, latent_dim:]
    key_total = source.shape[0]
    live_rows = jnp.arange(seq_len) < length
    cotangent = jnp.where(live_rows[:, None, None], out_grad, jnp.zeros_like(out_grad))
    block_rows = min(seq_len, 256)
    head_part = kv_up.shape[1]
    projected = jnp.einsum(
        "kl,lhd->khd", source_latent, kv_up, preferred_element_type=jnp.float32
    ).astype(jnp.bfloat16)
    key_nope = projected[:, :, :nope_dim]
    values = projected[:, :, nope_dim:]
    nope_total = jnp.zeros((key_total, head_part, nope_dim), jnp.float32)
    rope_total = jnp.zeros((key_total, rope_dim), jnp.float32)
    value_total = jnp.zeros((key_total, head_part, value_dim), jnp.float32)
    query_pieces = []
    for block_number in range(seq_len // block_rows):
        first_row = block_number * block_rows
        last_row = first_row + block_rows
        pieces = block_gradients(
            query_nope[first_row:last_row],
            query_rope[first_row:last_row],
            key_nope,
            key_rope,
            values,
            cotangent[first_row:last_row],
            first_row,
            length,
            prefix_rows,
        )
        nope_query, rope_query, nope_key, rope_key, value_grad = pieces
        nope_total = nope_total.at[:key_total].add(nope_key)
        rope_total = rope_total.at[:key_total].add(rope_key)
        value_total = value_total.at[:key_total].add(value_grad)
        query_pieces.append(
            jnp.concatenate(
                [
                    nope_query,
                    unrotate(
                        rope_query, cosine[first_row:last_row, None], sine[first_row:last_row, None]
                    ),
                ],
                axis=-1,
            ).astype(jnp.bfloat16)
        )
    head_projected_grad = jnp.concatenate([nope_total, value_total], axis=-1).astype(jnp.bfloat16)
    up_part = jnp.einsum(
        "kl,khd->lhd", source_latent, head_projected_grad, preferred_element_type=jnp.float32
    )
    query_grad, projected_grad, rope_grad, up_part = (
        jnp.concatenate(query_pieces, axis=0),
        head_projected_grad,
        rope_total,
        up_part,
    )
    dp_size = lax.axis_size("dp")
    head_size = lax.axis_size("head")
    up_pieces = lax.all_to_all(
        up_part.astype(jnp.bfloat16).reshape((dp_size, -1) + up_part.shape[1:]), "dp", 0, 0, tiled=False
    )
    up_grad = jnp.sum(up_pieces.astype(jnp.float32), axis=0)
    token_grad = projected_grad[prefix_rows:]
    token_rope_grad = rope_grad[prefix_rows:]
    latent_part = jnp.einsum("khd,lhd->kl", token_grad, kv_up, preferred_element_type=jnp.float32)
    token_part = jnp.concatenate(
        [latent_part, unrotate(token_rope_grad, cosine, sine)], axis=1
    ).astype(jnp.bfloat16)
    token_pieces = lax.all_to_all(
        token_part.reshape((head_size, -1) + token_part.shape[1:]), "head", 0, 0, tiled=False
    )
    latent_grad = jnp.sum(token_pieces.astype(jnp.float32), axis=0)
    latent_part = jnp.einsum(
        "khd,lhd->kl", projected_grad[:prefix_rows], kv_up, preferred_element_type=jnp.float32
    )
    prefix_part = jnp.concatenate([latent_part, rope_grad[:prefix_rows]], axis=1)
    world = dp_size * head_size
    prefix_pieces = lax.all_to_all(
        prefix_part.reshape((world, -1) + prefix_part.shape[1:]), ("dp", "head"), 0, 0, tiled=False
    )
    prefix_own = jnp.sum(prefix_pieces, axis=0)
    prefix_copies = jnp.broadcast_to(prefix_own[None], (world,) + prefix_own.shape)
    prefix_grad = lax.all_to_all(prefix_copies, ("dp", "head"), 0, 0, tiled=False).reshape(
        prefix_part.shape
    )
    return (query_grad, latent_grad, up_grad, prefix_grad)


def solution(mesh):
    placed = (
        P("dp", "head", None),
        P("dp", None),
        P(),
        P(None, "head", None),
        P("dp", "head", None),
        P("dp"),
        P("dp", None),
    )
    return jax.shard_map(
        on_device,
        mesh=mesh,
        in_specs=placed,
        out_specs=(P("dp", "head", None), P(("dp", "head"), None), P("dp", "head", None), P()),
        check_vma=False,
    )
```

```python
import jax
import jax.numpy as jnp
from jax import lax
from jax.sharding import Mesh, PartitionSpec as P


def angles_of(positions, rope_dim):
    halfway = rope_dim // 2
    frequency = 10000.0 ** (-(jnp.arange(halfway, dtype=jnp.float32) * 2.0 / rope_dim))
    angles = positions.astype(jnp.float32)[:, None] * frequency[None, :]
    return (jnp.cos(angles), jnp.sin(angles))


def rotate(values, cosine, sine):
    halfway = values.shape[-1] // 2
    leading = values[..., :halfway]
    trailing = values[..., halfway:]
    return jnp.concatenate(
        [leading * cosine - trailing * sine, trailing * cosine + leading * sine], axis=-1
    )


def unrotate(values, cosine, sine):
    halfway = values.shape[-1] // 2
    leading = values[..., :halfway]
    trailing = values[..., halfway:]
    return jnp.concatenate(
        [leading * cosine + trailing * sine, trailing * cosine - leading * sine], axis=-1
    )


def block_gradients(
    query_nope, query_rope, key_nope, key_rope, values, cotangent, first_row, length, prefix_rows
):
    score_scale = (query_nope.shape[-1] + query_rope.shape[-1]) ** (-0.5)
    scores = (
        jnp.einsum("qhd,khd->hqk", query_nope, key_nope, preferred_element_type=jnp.float32)
        + jnp.einsum("qhr,kr->hqk", query_rope, key_rope, preferred_element_type=jnp.float32)
    ) * score_scale
    row_index = first_row + jnp.arange(query_nope.shape[0])
    col_index = jnp.arange(key_nope.shape[0]) - prefix_rows
    allowed = (col_index[None, :] < 0) | (col_index[None, :] <= row_index[:, None]) & (
        col_index[None, :] < length
    )
    scores = jnp.where(allowed[None], scores, -jnp.inf)
    highest = jnp.max(scores, axis=-1, keepdims=True)
    exponent = jnp.exp(scores - highest)
    probability = exponent / jnp.sum(exponent, axis=-1, keepdims=True)
    weights = probability.astype(jnp.bfloat16)
    output = jnp.einsum("hqk,khv->qhv", weights, values, preferred_element_type=jnp.float32)
    row_delta = jnp.sum(cotangent.astype(jnp.float32) * output, axis=-1)
    prob_grad = jnp.einsum("qhv,khv->hqk", cotangent, values, preferred_element_type=jnp.float32)
    score_grad = (
        probability * (prob_grad - jnp.transpose(row_delta)[:, :, None]) * score_scale
    ).astype(jnp.bfloat16)
    nope_query = jnp.einsum(
        "hqk,khd->qhd", score_grad, key_nope, preferred_element_type=jnp.float32
    )
    rope_query = jnp.einsum("hqk,kr->qhr", score_grad, key_rope, preferred_element_type=jnp.float32)
    nope_key = jnp.einsum(
        "hqk,qhd->khd", score_grad, query_nope, preferred_element_type=jnp.float32
    )
    rope_key = jnp.einsum("hqk,qhr->kr", score_grad, query_rope, preferred_element_type=jnp.float32)
    value_grad = jnp.einsum("hqk,qhv->khv", weights, cotangent, preferred_element_type=jnp.float32)
    return (nope_query, rope_query, nope_key, rope_key, value_grad)


def swap_pair(values):
    return lax.ppermute(values, "core", [(0, 1), (1, 0)])


def on_device(queries, latent, prefix, kv_up, out_grad, lengths, positions):
    seq_len = queries.shape[0]
    latent_dim = kv_up.shape[0]
    value_dim = out_grad.shape[2]
    nope_dim = kv_up.shape[2] - value_dim
    rope_dim = latent.shape[1] - latent_dim
    prefix_rows = prefix.shape[0]
    length = lengths[0]
    cosine, sine = angles_of(positions[0], rope_dim)
    query_nope = queries[:, :, :nope_dim]
    query_rope = rotate(
        queries[:, :, nope_dim:].astype(jnp.float32), cosine[:, None], sine[:, None]
    ).astype(jnp.bfloat16)
    token_rope = rotate(latent[:, latent_dim:].astype(jnp.float32), cosine, sine).astype(
        jnp.bfloat16
    )
    source = jnp.concatenate(
        [prefix, jnp.concatenate([latent[:, :latent_dim], token_rope], axis=1)], axis=0
    )
    source_latent = source[:, :latent_dim]
    key_rope = source[:, latent_dim:]
    key_total = source.shape[0]
    live_rows = jnp.arange(seq_len) < length
    cotangent = jnp.where(live_rows[:, None, None], out_grad, jnp.zeros_like(out_grad))
    block_rows = min(seq_len, 256)
    head_part = kv_up.shape[1]
    projected = jnp.einsum(
        "kl,lhd->khd", source_latent, kv_up, preferred_element_type=jnp.float32
    ).astype(jnp.bfloat16)
    key_nope = projected[:, :, :nope_dim]
    values = projected[:, :, nope_dim:]
    nope_total = jnp.zeros((key_total, head_part, nope_dim), jnp.float32)
    rope_total = jnp.zeros((key_total, rope_dim), jnp.float32)
    value_total = jnp.zeros((key_total, head_part, value_dim), jnp.float32)
    query_pieces = []
    for block_number in range(seq_len // block_rows):
        first_row = block_number * block_rows
        last_row = first_row + block_rows
        seen = prefix_rows + last_row
        pieces = block_gradients(
            query_nope[first_row:last_row],
            query_rope[first_row:last_row],
            key_nope[:seen],
            key_rope[:seen],
            values[:seen],
            cotangent[first_row:last_row],
            first_row,
            length,
            prefix_rows,
        )
        nope_query, rope_query, nope_key, rope_key, value_grad = pieces
        nope_total = nope_total.at[:seen].add(nope_key)
        rope_total = rope_total.at[:seen].add(rope_key)
        value_total = value_total.at[:seen].add(value_grad)
        query_pieces.append(
            jnp.concatenate(
                [
                    nope_query,
                    unrotate(
                        rope_query, cosine[first_row:last_row, None], sine[first_row:last_row, None]
                    ),
                ],
                axis=-1,
            ).astype(jnp.bfloat16)
        )
    head_projected_grad = jnp.concatenate([nope_total, value_total], axis=-1).astype(jnp.bfloat16)
    up_part = jnp.einsum(
        "kl,khd->lhd", source_latent, head_projected_grad, preferred_element_type=jnp.float32
    )
    query_grad, projected_grad, rope_grad, up_part = (
        jnp.concatenate(query_pieces, axis=0),
        head_projected_grad,
        rope_total,
        up_part,
    )
    dp_size = lax.axis_size("dp")
    up_pieces = lax.all_to_all(
        up_part.astype(jnp.bfloat16).reshape((dp_size, -1) + up_part.shape[1:]), "dp", 0, 0, tiled=False
    )
    up_grad = jnp.sum(up_pieces.astype(jnp.float32), axis=0)
    token_grad = projected_grad[prefix_rows:]
    token_rope_grad = rope_grad[prefix_rows:]
    latent_part = jnp.einsum("khd,lhd->kl", token_grad, kv_up, preferred_element_type=jnp.float32)
    token_part = jnp.concatenate(
        [latent_part, unrotate(token_rope_grad, cosine, sine)], axis=1
    ).astype(jnp.bfloat16)
    core = lax.axis_index("core")
    pair_size = lax.axis_size("core")
    row_size = lax.axis_size("hr")
    token_blocks = token_part.reshape((row_size, pair_size, -1) + token_part.shape[1:])
    token_mine = jnp.where(core == 0, token_blocks[:, 0], token_blocks[:, 1])
    token_other = jnp.where(core == 0, token_blocks[:, 1], token_blocks[:, 0])
    token_pair = (
        token_mine.astype(jnp.float32) + swap_pair(token_other).astype(jnp.float32)
    ).astype(jnp.bfloat16)
    token_pieces = lax.all_to_all(token_pair, "hr", 0, 0, tiled=False)
    latent_grad = jnp.sum(token_pieces.astype(jnp.float32), axis=0)
    latent_part = jnp.einsum(
        "khd,lhd->kl", projected_grad[:prefix_rows], kv_up, preferred_element_type=jnp.float32
    )
    prefix_part = jnp.concatenate([latent_part, rope_grad[:prefix_rows]], axis=1)
    half_rows = prefix_part.shape[0] // 2
    prefix_mine = lax.dynamic_slice_in_dim(prefix_part, core * half_rows, half_rows)
    prefix_other = lax.dynamic_slice_in_dim(prefix_part, (1 - core) * half_rows, half_rows)
    prefix_half = prefix_mine + swap_pair(prefix_other)
    outer = ("dp", "hr")
    outer_size = dp_size * row_size
    prefix_pieces = lax.all_to_all(
        prefix_half.reshape((outer_size, -1) + prefix_half.shape[1:]), outer, 0, 0, tiled=False
    )
    prefix_own = jnp.sum(prefix_pieces, axis=0)
    prefix_copies = jnp.broadcast_to(prefix_own[None], (outer_size,) + prefix_own.shape)
    prefix_gathered = lax.all_to_all(prefix_copies, outer, 0, 0, tiled=False).reshape(
        prefix_half.shape
    )
    prefix_partner = swap_pair(prefix_gathered)
    prefix_grad = jnp.where(
        core == 0,
        jnp.concatenate([prefix_gathered, prefix_partner], axis=0),
        jnp.concatenate([prefix_partner, prefix_gathered], axis=0),
    )
    return (query_grad, latent_grad, up_grad, prefix_grad)


def solution(mesh):
    dp_size, head_size = mesh.shape["dp"], mesh.shape["head"]
    split = Mesh(mesh.devices.reshape(dp_size, head_size // 2, 2), ("dp", "hr", "core"))
    head = ("hr", "core")
    placed = (
        P("dp", head, None),
        P("dp", None),
        P(),
        P(None, head, None),
        P("dp", head, None),
        P("dp"),
        P("dp", None),
    )
    return jax.shard_map(
        on_device,
        mesh=split,
        in_specs=placed,
        out_specs=(P("dp", head, None), P(("dp",) + head, None), P("dp", head, None), P()),
        check_vma=False,
    )
```

```python
import jax
import jax.numpy as jnp
from jax import lax
from jax.sharding import Mesh, PartitionSpec as P


def angles_of(positions, rope_dim):
    halfway = rope_dim // 2
    frequency = 10000.0 ** (-(jnp.arange(halfway, dtype=jnp.float32) * 2.0 / rope_dim))
    angles = positions.astype(jnp.float32)[:, None] * frequency[None, :]
    return (jnp.cos(angles), jnp.sin(angles))


def rotate(values, cosine, sine):
    halfway = values.shape[-1] // 2
    leading = values[..., :halfway]
    trailing = values[..., halfway:]
    return jnp.concatenate(
        [leading * cosine - trailing * sine, trailing * cosine + leading * sine], axis=-1
    )


def unrotate(values, cosine, sine):
    halfway = values.shape[-1] // 2
    leading = values[..., :halfway]
    trailing = values[..., halfway:]
    return jnp.concatenate(
        [leading * cosine + trailing * sine, trailing * cosine - leading * sine], axis=-1
    )


def block_gradients(
    query_nope, query_rope, key_nope, key_rope, values, cotangent, first_row, length, prefix_rows
):
    score_scale = (query_nope.shape[-1] + query_rope.shape[-1]) ** (-0.5)
    scores = (
        jnp.einsum("qhd,khd->hqk", query_nope, key_nope, preferred_element_type=jnp.float32)
        + jnp.einsum("qhr,kr->hqk", query_rope, key_rope, preferred_element_type=jnp.float32)
    ) * score_scale
    row_index = first_row + jnp.arange(query_nope.shape[0])
    col_index = jnp.arange(key_nope.shape[0]) - prefix_rows
    allowed = (col_index[None, :] < 0) | (col_index[None, :] <= row_index[:, None]) & (
        col_index[None, :] < length
    )
    scores = jnp.where(allowed[None], scores, -jnp.inf)
    highest = jnp.max(scores, axis=-1, keepdims=True)
    exponent = jnp.exp(scores - highest)
    probability = exponent / jnp.sum(exponent, axis=-1, keepdims=True)
    weights = probability.astype(jnp.bfloat16)
    output = jnp.einsum("hqk,khv->qhv", weights, values, preferred_element_type=jnp.float32)
    row_delta = jnp.sum(cotangent.astype(jnp.float32) * output, axis=-1)
    prob_grad = jnp.einsum("qhv,khv->hqk", cotangent, values, preferred_element_type=jnp.float32)
    score_grad = (
        probability * (prob_grad - jnp.transpose(row_delta)[:, :, None]) * score_scale
    ).astype(jnp.bfloat16)
    nope_query = jnp.einsum(
        "hqk,khd->qhd", score_grad, key_nope, preferred_element_type=jnp.float32
    )
    rope_query = jnp.einsum("hqk,kr->qhr", score_grad, key_rope, preferred_element_type=jnp.float32)
    nope_key = jnp.einsum(
        "hqk,qhd->khd", score_grad, query_nope, preferred_element_type=jnp.float32
    )
    rope_key = jnp.einsum("hqk,qhr->kr", score_grad, query_rope, preferred_element_type=jnp.float32)
    value_grad = jnp.einsum("hqk,qhv->khv", weights, cotangent, preferred_element_type=jnp.float32)
    return (nope_query, rope_query, nope_key, rope_key, value_grad)


def swap_pair(values):
    return lax.ppermute(values, "core", [(0, 1), (1, 0)])


def gather_copies(values, axis, size):
    copies = jnp.broadcast_to(values[None], (size,) + values.shape)
    gathered = lax.all_to_all(copies, axis, 0, 0, tiled=False)
    return gathered.reshape((size * values.shape[0],) + values.shape[1:])


def on_device(queries, latent, prefix, kv_up, out_grad, lengths, positions):
    seq_len = queries.shape[0]
    latent_dim = kv_up.shape[0]
    value_dim = out_grad.shape[2]
    nope_dim = kv_up.shape[2] - value_dim
    rope_dim = latent.shape[1] - latent_dim
    prefix_rows = prefix.shape[0]
    length = lengths[0]
    cosine, sine = angles_of(positions[0], rope_dim)
    query_nope = queries[:, :, :nope_dim]
    query_rope = rotate(
        queries[:, :, nope_dim:].astype(jnp.float32), cosine[:, None], sine[:, None]
    ).astype(jnp.bfloat16)
    token_rope = rotate(latent[:, latent_dim:].astype(jnp.float32), cosine, sine).astype(
        jnp.bfloat16
    )
    source = jnp.concatenate(
        [prefix, jnp.concatenate([latent[:, :latent_dim], token_rope], axis=1)], axis=0
    )
    source_latent = source[:, :latent_dim]
    key_rope = source[:, latent_dim:]
    key_total = source.shape[0]
    live_rows = jnp.arange(seq_len) < length
    cotangent = jnp.where(live_rows[:, None, None], out_grad, jnp.zeros_like(out_grad))
    block_rows = min(seq_len, 256)
    head_part = kv_up.shape[1]
    projected = jnp.einsum(
        "kl,lhd->khd", source_latent, kv_up, preferred_element_type=jnp.float32
    ).astype(jnp.bfloat16)
    key_nope = projected[:, :, :nope_dim]
    values = projected[:, :, nope_dim:]
    nope_total = jnp.zeros((key_total, head_part, nope_dim), jnp.float32)
    rope_total = jnp.zeros((key_total, rope_dim), jnp.float32)
    value_total = jnp.zeros((key_total, head_part, value_dim), jnp.float32)
    query_pieces = []
    for block_number in range(seq_len // block_rows):
        first_row = block_number * block_rows
        last_row = first_row + block_rows
        seen = prefix_rows + last_row
        pieces = block_gradients(
            query_nope[first_row:last_row],
            query_rope[first_row:last_row],
            key_nope[:seen],
            key_rope[:seen],
            values[:seen],
            cotangent[first_row:last_row],
            first_row,
            length,
            prefix_rows,
        )
        nope_query, rope_query, nope_key, rope_key, value_grad = pieces
        nope_total = nope_total.at[:seen].add(nope_key)
        rope_total = rope_total.at[:seen].add(rope_key)
        value_total = value_total.at[:seen].add(value_grad)
        query_pieces.append(
            jnp.concatenate(
                [
                    nope_query,
                    unrotate(
                        rope_query, cosine[first_row:last_row, None], sine[first_row:last_row, None]
                    ),
                ],
                axis=-1,
            ).astype(jnp.bfloat16)
        )
    head_projected_grad = jnp.concatenate([nope_total, value_total], axis=-1).astype(jnp.bfloat16)
    up_part = jnp.einsum(
        "kl,khd->lhd", source_latent, head_projected_grad, preferred_element_type=jnp.float32
    )
    query_grad, projected_grad, rope_grad, up_part = (
        jnp.concatenate(query_pieces, axis=0),
        head_projected_grad,
        rope_total,
        up_part,
    )
    dp_size = lax.axis_size("dp")
    up_pieces = lax.all_to_all(
        up_part.astype(jnp.bfloat16).reshape((dp_size, -1) + up_part.shape[1:]), "dp", 0, 0, tiled=False
    )
    up_grad = jnp.sum(up_pieces.astype(jnp.float32), axis=0)
    token_grad = projected_grad[prefix_rows:]
    token_rope_grad = rope_grad[prefix_rows:]
    latent_part = jnp.einsum("khd,lhd->kl", token_grad, kv_up, preferred_element_type=jnp.float32)
    token_part = jnp.concatenate(
        [latent_part, unrotate(token_rope_grad, cosine, sine)], axis=1
    ).astype(jnp.bfloat16)
    core = lax.axis_index("core")
    pair_size = lax.axis_size("core")
    row_size = lax.axis_size("hr")
    token_blocks = token_part.reshape((row_size, pair_size, -1) + token_part.shape[1:])
    token_mine = jnp.where(core == 0, token_blocks[:, 0], token_blocks[:, 1])
    token_other = jnp.where(core == 0, token_blocks[:, 1], token_blocks[:, 0])
    token_pair = (
        token_mine.astype(jnp.float32) + swap_pair(token_other).astype(jnp.float32)
    ).astype(jnp.bfloat16)
    token_pieces = lax.all_to_all(token_pair, "hr", 0, 0, tiled=False)
    latent_grad = jnp.sum(token_pieces.astype(jnp.float32), axis=0)
    latent_part = jnp.einsum(
        "khd,lhd->kl", projected_grad[:prefix_rows], kv_up, preferred_element_type=jnp.float32
    )
    prefix_part = jnp.concatenate([latent_part, rope_grad[:prefix_rows]], axis=1)
    half_rows = prefix_part.shape[0] // 2
    prefix_mine = lax.dynamic_slice_in_dim(prefix_part, core * half_rows, half_rows)
    prefix_other = lax.dynamic_slice_in_dim(prefix_part, (1 - core) * half_rows, half_rows)
    prefix_half = prefix_mine + swap_pair(prefix_other)
    prefix_rows_part = jnp.sum(
        lax.all_to_all(
            prefix_half.reshape((row_size, -1) + prefix_half.shape[1:]), "hr", 0, 0, tiled=False
        ),
        axis=0,
    )
    prefix_own = jnp.sum(
        lax.all_to_all(
            prefix_rows_part.reshape((dp_size, -1) + prefix_rows_part.shape[1:]),
            "dp",
            0,
            0,
            tiled=False,
        ),
        axis=0,
    )
    prefix_rows_full = gather_copies(prefix_own, "dp", dp_size)
    prefix_gathered = gather_copies(prefix_rows_full, "hr", row_size)
    prefix_partner = swap_pair(prefix_gathered)
    prefix_grad = jnp.where(
        core == 0,
        jnp.concatenate([prefix_gathered, prefix_partner], axis=0),
        jnp.concatenate([prefix_partner, prefix_gathered], axis=0),
    )
    return (query_grad, latent_grad, up_grad, prefix_grad)


def solution(mesh):
    dp_size, head_size = mesh.shape["dp"], mesh.shape["head"]
    split = Mesh(mesh.devices.reshape(dp_size, head_size // 2, 2), ("dp", "hr", "core"))
    head = ("hr", "core")
    placed = (
        P("dp", head, None),
        P("dp", None),
        P(),
        P(None, head, None),
        P("dp", head, None),
        P("dp"),
        P("dp", None),
    )
    return jax.shard_map(
        on_device,
        mesh=split,
        in_specs=placed,
        out_specs=(P("dp", head, None), P(("dp",) + head, None), P("dp", head, None), P()),
        check_vma=False,
    )
```

```python
import jax
import jax.numpy as jnp
from jax import lax
from jax.sharding import Mesh, PartitionSpec as P


def angles_of(positions, rope_dim):
    halfway = rope_dim // 2
    frequency = 10000.0 ** (-(jnp.arange(halfway, dtype=jnp.float32) * 2.0 / rope_dim))
    angles = positions.astype(jnp.float32)[:, None] * frequency[None, :]
    return (jnp.cos(angles), jnp.sin(angles))


def rotate(values, cosine, sine):
    halfway = values.shape[-1] // 2
    leading = values[..., :halfway]
    trailing = values[..., halfway:]
    return jnp.concatenate(
        [leading * cosine - trailing * sine, trailing * cosine + leading * sine], axis=-1
    )


def unrotate(values, cosine, sine):
    halfway = values.shape[-1] // 2
    leading = values[..., :halfway]
    trailing = values[..., halfway:]
    return jnp.concatenate(
        [leading * cosine + trailing * sine, trailing * cosine - leading * sine], axis=-1
    )


def block_gradients(
    query_nope, query_rope, key_nope, key_rope, values, cotangent, first_row, length, prefix_rows
):
    score_scale = (query_nope.shape[-1] + query_rope.shape[-1]) ** (-0.5)
    scores = (
        jnp.einsum("qhd,khd->hqk", query_nope, key_nope, preferred_element_type=jnp.float32)
        + jnp.einsum("qhr,kr->hqk", query_rope, key_rope, preferred_element_type=jnp.float32)
    ) * score_scale
    row_index = first_row + jnp.arange(query_nope.shape[0])
    col_index = jnp.arange(key_nope.shape[0]) - prefix_rows
    allowed = (col_index[None, :] < 0) | (col_index[None, :] <= row_index[:, None]) & (
        col_index[None, :] < length
    )
    scores = jnp.where(allowed[None], scores, -jnp.inf)
    highest = jnp.max(scores, axis=-1, keepdims=True)
    exponent = jnp.exp(scores - highest)
    probability = exponent / jnp.sum(exponent, axis=-1, keepdims=True)
    weights = probability.astype(jnp.bfloat16)
    output = jnp.einsum("hqk,khv->qhv", weights, values, preferred_element_type=jnp.float32)
    row_delta = jnp.sum(cotangent.astype(jnp.float32) * output, axis=-1)
    prob_grad = jnp.einsum("qhv,khv->hqk", cotangent, values, preferred_element_type=jnp.float32)
    score_grad = (
        probability * (prob_grad - jnp.transpose(row_delta)[:, :, None]) * score_scale
    ).astype(jnp.bfloat16)
    nope_query = jnp.einsum(
        "hqk,khd->qhd", score_grad, key_nope, preferred_element_type=jnp.float32
    )
    rope_query = jnp.einsum("hqk,kr->qhr", score_grad, key_rope, preferred_element_type=jnp.float32)
    return (nope_query, rope_query, score_grad, weights)


def key_gradients(score_grads, weights, query_nopes, query_ropes, cotangents, first, last):
    nope_key = rope_key = value_grad = None
    for score_grad, weight, query_nope, query_rope, cotangent in zip(
        score_grads, weights, query_nopes, query_ropes, cotangents
    ):
        if score_grad.shape[-1] < last:
            continue
        part = score_grad[:, :, first:last]
        nope = jnp.einsum("hqk,qhd->khd", part, query_nope, preferred_element_type=jnp.float32)
        rope = jnp.einsum("hqk,qhr->kr", part, query_rope, preferred_element_type=jnp.float32)
        value = jnp.einsum(
            "hqk,qhv->khv", weight[:, :, first:last], cotangent, preferred_element_type=jnp.float32
        )
        if nope_key is None:
            nope_key, rope_key, value_grad = nope, rope, value
        else:
            nope_key, rope_key, value_grad = nope_key + nope, rope_key + rope, value_grad + value
    return nope_key, rope_key, value_grad


def swap_pair(values):
    return lax.ppermute(values, "core", [(0, 1), (1, 0)])


def device_step(queries, latent, prefix, kv_up, out_grad, lengths, positions):
    seq_len = queries.shape[0]
    latent_dim = kv_up.shape[0]
    value_dim = out_grad.shape[2]
    nope_dim = kv_up.shape[2] - value_dim
    rope_dim = latent.shape[1] - latent_dim
    prefix_rows = prefix.shape[0]
    length = lengths[0]
    cosine, sine = angles_of(positions[0], rope_dim)
    query_nope = queries[:, :, :nope_dim]
    query_rope = rotate(
        queries[:, :, nope_dim:].astype(jnp.float32), cosine[:, None], sine[:, None]
    ).astype(jnp.bfloat16)
    token_rope = rotate(latent[:, latent_dim:].astype(jnp.float32), cosine, sine).astype(
        jnp.bfloat16
    )
    source = jnp.concatenate(
        [prefix, jnp.concatenate([latent[:, :latent_dim], token_rope], axis=1)], axis=0
    )
    source_latent = source[:, :latent_dim]
    key_rope = source[:, latent_dim:]
    live_rows = jnp.arange(seq_len) < length
    cotangent = jnp.where(live_rows[:, None, None], out_grad, jnp.zeros_like(out_grad))
    block_rows = min(seq_len, 256)
    projected = jnp.einsum(
        "kl,lhd->khd", source_latent, kv_up, preferred_element_type=jnp.float32
    ).astype(jnp.bfloat16)
    key_nope = projected[:, :, :nope_dim]
    values = projected[:, :, nope_dim:]
    query_pieces = []
    score_grads, weight_blocks, nope_blocks, rope_blocks, cot_blocks = [], [], [], [], []
    for block_number in range(seq_len // block_rows):
        first_row = block_number * block_rows
        last_row = first_row + block_rows
        seen = prefix_rows + last_row
        nope_block = query_nope[first_row:last_row]
        rope_block = query_rope[first_row:last_row]
        cot_block = cotangent[first_row:last_row]
        nope_query, rope_query, score_grad, weights = block_gradients(
            nope_block,
            rope_block,
            key_nope[:seen],
            key_rope[:seen],
            values[:seen],
            cot_block,
            first_row,
            length,
            prefix_rows,
        )
        score_grads.append(score_grad)
        weight_blocks.append(weights)
        nope_blocks.append(nope_block)
        rope_blocks.append(rope_block)
        cot_blocks.append(cot_block)
        query_pieces.append(
            jnp.concatenate(
                [
                    nope_query,
                    unrotate(
                        rope_query, cosine[first_row:last_row, None], sine[first_row:last_row, None]
                    ),
                ],
                axis=-1,
            ).astype(jnp.bfloat16)
        )
    key_inputs = (score_grads, weight_blocks, nope_blocks, rope_blocks, cot_blocks)
    nope_prefix, rope_prefix, value_prefix = key_gradients(*key_inputs, 0, prefix_rows)
    prefix_projected_grad = jnp.concatenate([nope_prefix, value_prefix], axis=-1).astype(jnp.bfloat16)
    token_sets = []
    for block_number in range(seq_len // block_rows):
        first = prefix_rows + block_number * block_rows
        token_sets.append(key_gradients(*key_inputs, first, first + block_rows))
    nope_total = jnp.concatenate([nope_prefix] + [t[0] for t in token_sets], axis=0)
    rope_total = jnp.concatenate([rope_prefix] + [t[1] for t in token_sets], axis=0)
    value_total = jnp.concatenate([value_prefix] + [t[2] for t in token_sets], axis=0)
    head_projected_grad = jnp.concatenate([nope_total, value_total], axis=-1).astype(jnp.bfloat16)
    up_part = jnp.einsum(
        "kl,khd->lhd", source_latent, head_projected_grad, preferred_element_type=jnp.float32
    )
    query_grad = jnp.concatenate(query_pieces, axis=0)
    projected_grad = head_projected_grad
    rope_grad = rope_total
    dp_size = lax.axis_size("dp")
    up_pieces = lax.all_to_all(
        up_part.astype(jnp.bfloat16).reshape((dp_size, -1) + up_part.shape[1:]), "dp", 0, 0, tiled=False
    )
    up_grad = jnp.sum(up_pieces.astype(jnp.float32), axis=0)
    token_grad = projected_grad[prefix_rows:]
    token_rope_grad = rope_grad[prefix_rows:]
    latent_part = jnp.einsum("khd,lhd->kl", token_grad, kv_up, preferred_element_type=jnp.float32)
    token_part = jnp.concatenate(
        [latent_part, unrotate(token_rope_grad, cosine, sine)], axis=1
    ).astype(jnp.bfloat16)
    core = lax.axis_index("core")
    pair_size = lax.axis_size("core")
    row_size = lax.axis_size("hr")
    token_blocks = token_part.reshape((row_size, pair_size, -1) + token_part.shape[1:])
    token_mine = jnp.where(core == 0, token_blocks[:, 0], token_blocks[:, 1])
    token_other = jnp.where(core == 0, token_blocks[:, 1], token_blocks[:, 0])
    token_pair = (
        token_mine.astype(jnp.float32) + swap_pair(token_other).astype(jnp.float32)
    ).astype(jnp.bfloat16)
    token_pieces = lax.all_to_all(token_pair, "hr", 0, 0, tiled=False)
    latent_grad = jnp.sum(token_pieces.astype(jnp.float32), axis=0)
    latent_part = jnp.einsum(
        "khd,lhd->kl", prefix_projected_grad, kv_up, preferred_element_type=jnp.float32
    )
    prefix_part = jnp.concatenate([latent_part, rope_grad[:prefix_rows]], axis=1)
    half_rows = prefix_part.shape[0] // 2
    prefix_mine = lax.dynamic_slice_in_dim(prefix_part, core * half_rows, half_rows)
    prefix_other = lax.dynamic_slice_in_dim(prefix_part, (1 - core) * half_rows, half_rows)
    prefix_half = prefix_mine + swap_pair(prefix_other)
    outer = ("dp", "hr")
    outer_size = dp_size * row_size
    prefix_pieces = lax.all_to_all(
        prefix_half.reshape((outer_size, -1) + prefix_half.shape[1:]), outer, 0, 0, tiled=False
    )
    prefix_own = jnp.sum(prefix_pieces, axis=0)
    prefix_copies = jnp.broadcast_to(prefix_own[None], (outer_size,) + prefix_own.shape)
    prefix_gathered = lax.all_to_all(prefix_copies, outer, 0, 0, tiled=False).reshape(
        prefix_half.shape
    )
    prefix_partner = swap_pair(prefix_gathered)
    prefix_grad = jnp.where(
        core == 0,
        jnp.concatenate([prefix_gathered, prefix_partner], axis=0),
        jnp.concatenate([prefix_partner, prefix_gathered], axis=0),
    )
    return (query_grad, latent_grad, up_grad, prefix_grad)


def solution(mesh):
    dp_size, head_size = mesh.shape["dp"], mesh.shape["head"]
    split = Mesh(mesh.devices.reshape(dp_size, head_size // 2, 2), ("dp", "hr", "core"))
    head = ("hr", "core")
    placed = (
        P("dp", head, None),
        P("dp", None),
        P(),
        P(None, head, None),
        P("dp", head, None),
        P("dp"),
        P("dp", None),
    )
    return jax.shard_map(
        device_step,
        mesh=split,
        in_specs=placed,
        out_specs=(P("dp", head, None), P(("dp",) + head, None), P("dp", head, None), P()),
        check_vma=False,
    )
```

```python
import jax
import jax.numpy as jnp
from jax import lax
from jax.sharding import Mesh, PartitionSpec as P


def angles_of(positions, rope_dim):
    halfway = rope_dim // 2
    frequency = 10000.0 ** (-(jnp.arange(halfway, dtype=jnp.float32) * 2.0 / rope_dim))
    angles = positions.astype(jnp.float32)[:, None] * frequency[None, :]
    return (jnp.cos(angles), jnp.sin(angles))


def rotate(values, cosine, sine):
    halfway = values.shape[-1] // 2
    leading = values[..., :halfway]
    trailing = values[..., halfway:]
    return jnp.concatenate(
        [leading * cosine - trailing * sine, trailing * cosine + leading * sine], axis=-1
    )


def unrotate(values, cosine, sine):
    halfway = values.shape[-1] // 2
    leading = values[..., :halfway]
    trailing = values[..., halfway:]
    return jnp.concatenate(
        [leading * cosine + trailing * sine, trailing * cosine - leading * sine], axis=-1
    )


def block_gradients(
    query_nope, query_rope, key_nope, key_rope, values, cotangent, first_row, length, prefix_rows
):
    score_scale = (query_nope.shape[-1] + query_rope.shape[-1]) ** (-0.5)
    scores = (
        jnp.einsum("qhd,khd->hqk", query_nope, key_nope, preferred_element_type=jnp.float32)
        + jnp.einsum("qhr,kr->hqk", query_rope, key_rope, preferred_element_type=jnp.float32)
    ) * score_scale
    row_index = first_row + jnp.arange(query_nope.shape[0])
    col_index = jnp.arange(key_nope.shape[0]) - prefix_rows
    allowed = (col_index[None, :] < 0) | (col_index[None, :] <= row_index[:, None]) & (
        col_index[None, :] < length
    )
    scores = jnp.where(allowed[None], scores, -jnp.inf)
    highest = jnp.max(scores, axis=-1, keepdims=True)
    exponent = jnp.exp(scores - highest)
    probability = exponent / jnp.sum(exponent, axis=-1, keepdims=True)
    weights = probability.astype(jnp.bfloat16)
    output = jnp.einsum("hqk,khv->qhv", weights, values, preferred_element_type=jnp.float32)
    row_delta = jnp.sum(cotangent.astype(jnp.float32) * output, axis=-1)
    prob_grad = jnp.einsum("qhv,khv->hqk", cotangent, values, preferred_element_type=jnp.float32)
    score_grad = (
        probability * (prob_grad - jnp.transpose(row_delta)[:, :, None]) * score_scale
    ).astype(jnp.bfloat16)
    nope_query = jnp.einsum(
        "hqk,khd->qhd", score_grad, key_nope, preferred_element_type=jnp.float32
    )
    rope_query = jnp.einsum("hqk,kr->qhr", score_grad, key_rope, preferred_element_type=jnp.float32)
    nope_key = jnp.einsum(
        "hqk,qhd->khd", score_grad, query_nope, preferred_element_type=jnp.float32
    )
    rope_key = jnp.einsum("hqk,qhr->kr", score_grad, query_rope, preferred_element_type=jnp.float32)
    value_grad = jnp.einsum("hqk,qhv->khv", weights, cotangent, preferred_element_type=jnp.float32)
    return (nope_query, rope_query, nope_key, rope_key, value_grad)


def swap_pair(values):
    return lax.ppermute(values, "core", [(0, 1), (1, 0)])


def device_step(queries, latent, prefix, kv_up, out_grad, lengths, positions):
    seq_len = queries.shape[0]
    latent_dim = kv_up.shape[0]
    value_dim = out_grad.shape[2]
    nope_dim = kv_up.shape[2] - value_dim
    rope_dim = latent.shape[1] - latent_dim
    prefix_rows = prefix.shape[0]
    length = lengths[0]
    cosine, sine = angles_of(positions[0], rope_dim)
    query_nope = queries[:, :, :nope_dim]
    query_rope = rotate(
        queries[:, :, nope_dim:].astype(jnp.float32), cosine[:, None], sine[:, None]
    ).astype(jnp.bfloat16)
    token_rope = rotate(latent[:, latent_dim:].astype(jnp.float32), cosine, sine).astype(
        jnp.bfloat16
    )
    source = jnp.concatenate(
        [prefix, jnp.concatenate([latent[:, :latent_dim], token_rope], axis=1)], axis=0
    )
    source_latent = source[:, :latent_dim]
    key_rope = source[:, latent_dim:]
    key_total = source.shape[0]
    live_rows = jnp.arange(seq_len) < length
    cotangent = jnp.where(live_rows[:, None, None], out_grad, jnp.zeros_like(out_grad))
    block_rows = min(seq_len, 256)
    head_part = kv_up.shape[1]
    projected = jnp.einsum(
        "kl,lhd->khd", source_latent, kv_up, preferred_element_type=jnp.float32
    ).astype(jnp.bfloat16)
    key_nope = projected[:, :, :nope_dim]
    values = projected[:, :, nope_dim:]
    nope_total = jnp.zeros((key_total, head_part, nope_dim), jnp.float32)
    rope_total = jnp.zeros((key_total, rope_dim), jnp.float32)
    value_total = jnp.zeros((key_total, head_part, value_dim), jnp.float32)
    query_pieces = []
    for block_number in range(seq_len // block_rows):
        first_row = block_number * block_rows
        last_row = first_row + block_rows
        seen = prefix_rows + last_row
        pieces = block_gradients(
            query_nope[first_row:last_row],
            query_rope[first_row:last_row],
            key_nope[:seen],
            key_rope[:seen],
            values[:seen],
            cotangent[first_row:last_row],
            first_row,
            length,
            prefix_rows,
        )
        nope_query, rope_query, nope_key, rope_key, value_grad = pieces
        nope_total = nope_total.at[:seen].add(nope_key)
        rope_total = rope_total.at[:seen].add(rope_key)
        value_total = value_total.at[:seen].add(value_grad)
        query_pieces.append(
            jnp.concatenate(
                [
                    nope_query,
                    unrotate(
                        rope_query,
                        cosine[first_row:last_row, None],
                        sine[first_row:last_row, None],
                    ),
                ],
                axis=-1,
            ).astype(jnp.bfloat16)
        )
    head_projected_grad = jnp.concatenate([nope_total, value_total], axis=-1).astype(jnp.bfloat16)
    up_part = jnp.einsum(
        "kl,khd->lhd", source_latent, head_projected_grad, preferred_element_type=jnp.float32
    )
    query_grad, projected_grad, rope_grad, up_part = (
        jnp.concatenate(query_pieces, axis=0),
        head_projected_grad,
        rope_total,
        up_part,
    )
    dp_size = lax.axis_size("dp")
    up_pieces = lax.all_to_all(
        up_part.astype(jnp.bfloat16).reshape((dp_size, -1) + up_part.shape[1:]), "dp", 0, 0, tiled=False
    )
    up_grad = jnp.sum(up_pieces.astype(jnp.float32), axis=0)
    token_grad = projected_grad[prefix_rows:]
    token_rope_grad = rope_grad[prefix_rows:]
    latent_part = jnp.einsum("khd,lhd->kl", token_grad, kv_up, preferred_element_type=jnp.float32)
    token_part = jnp.concatenate(
        [latent_part, unrotate(token_rope_grad, cosine, sine)], axis=1
    ).astype(jnp.bfloat16)
    core = lax.axis_index("core")
    pair_size = lax.axis_size("core")
    row_size = lax.axis_size("hr")
    token_blocks = token_part.reshape((row_size, pair_size, -1) + token_part.shape[1:])
    token_mine = jnp.where(core == 0, token_blocks[:, 0], token_blocks[:, 1])
    token_other = jnp.where(core == 0, token_blocks[:, 1], token_blocks[:, 0])
    token_pair = (
        token_mine.astype(jnp.float32) + swap_pair(token_other).astype(jnp.float32)
    ).astype(jnp.bfloat16)
    token_pieces = lax.all_to_all(token_pair, "hr", 0, 0, tiled=False)
    latent_grad = jnp.sum(token_pieces.astype(jnp.float32), axis=0)
    latent_part = jnp.einsum(
        "khd,lhd->kl", projected_grad[:prefix_rows], kv_up, preferred_element_type=jnp.float32
    )
    prefix_part = jnp.concatenate([latent_part, rope_grad[:prefix_rows]], axis=1)
    half_rows = prefix_part.shape[0] // 2
    prefix_mine = lax.dynamic_slice_in_dim(prefix_part, core * half_rows, half_rows)
    prefix_other = lax.dynamic_slice_in_dim(prefix_part, (1 - core) * half_rows, half_rows)
    prefix_half = prefix_mine + swap_pair(prefix_other)
    outer = ("dp", "hr")
    outer_size = dp_size * row_size
    prefix_pieces = lax.all_to_all(
        prefix_half.reshape((outer_size, -1) + prefix_half.shape[1:]), outer, 0, 0, tiled=False
    )
    prefix_own = jnp.sum(prefix_pieces, axis=0)
    prefix_copies = jnp.broadcast_to(prefix_own[None], (outer_size,) + prefix_own.shape)
    prefix_gathered = lax.all_to_all(prefix_copies, outer, 0, 0, tiled=False).reshape(
        prefix_half.shape
    )
    prefix_partner = swap_pair(prefix_gathered)
    prefix_grad = jnp.where(
        core == 0,
        jnp.concatenate([prefix_gathered, prefix_partner], axis=0),
        jnp.concatenate([prefix_partner, prefix_gathered], axis=0),
    )
    return (query_grad, latent_grad, up_grad, prefix_grad)


def solution(mesh):
    dp_size, head_size = mesh.shape["dp"], mesh.shape["head"]
    split = Mesh(mesh.devices.reshape(dp_size, head_size // 2, 2), ("dp", "hr", "core"))
    head = ("hr", "core")
    placed = (
        P("dp", head, None),
        P("dp", None),
        P(),
        P(None, head, None),
        P("dp", head, None),
        P("dp"),
        P("dp", None),
    )
    return jax.shard_map(
        device_step,
        mesh=split,
        in_specs=placed,
        out_specs=(P("dp", head, None), P(("dp",) + head, None), P("dp", head, None), P()),
        check_vma=False,
    )
```

```python
import jax
import jax.numpy as jnp
from jax import lax
from jax.sharding import Mesh, PartitionSpec as P


def angles_of(positions, rope_dim):
    halfway = rope_dim // 2
    frequency = 10000.0 ** (-(jnp.arange(halfway, dtype=jnp.float32) * 2.0 / rope_dim))
    angles = positions.astype(jnp.float32)[:, None] * frequency[None, :]
    return (jnp.cos(angles), jnp.sin(angles))


def rotate(values, cosine, sine):
    halfway = values.shape[-1] // 2
    leading = values[..., :halfway]
    trailing = values[..., halfway:]
    return jnp.concatenate(
        [leading * cosine - trailing * sine, trailing * cosine + leading * sine], axis=-1
    )


def unrotate(values, cosine, sine):
    halfway = values.shape[-1] // 2
    leading = values[..., :halfway]
    trailing = values[..., halfway:]
    return jnp.concatenate(
        [leading * cosine + trailing * sine, trailing * cosine - leading * sine], axis=-1
    )


def block_gradients(
    query_nope, query_rope, key_nope, key_rope, values, cotangent, first_row, length, prefix_rows
):
    score_scale = (query_nope.shape[-1] + query_rope.shape[-1]) ** (-0.5)
    scores = (
        jnp.einsum("qhd,khd->hqk", query_nope, key_nope, preferred_element_type=jnp.float32)
        + jnp.einsum("qhr,kr->hqk", query_rope, key_rope, preferred_element_type=jnp.float32)
    ) * score_scale
    row_index = first_row + jnp.arange(query_nope.shape[0])
    col_index = jnp.arange(key_nope.shape[0]) - prefix_rows
    allowed = (col_index[None, :] < 0) | (col_index[None, :] <= row_index[:, None]) & (
        col_index[None, :] < length
    )
    scores = jnp.where(allowed[None], scores, -jnp.inf)
    highest = jnp.max(scores, axis=-1, keepdims=True)
    exponent = jnp.exp(scores - highest)
    probability = exponent / jnp.sum(exponent, axis=-1, keepdims=True)
    weights = probability.astype(jnp.bfloat16)
    output = jnp.einsum("hqk,khv->qhv", weights, values, preferred_element_type=jnp.float32)
    row_delta = jnp.sum(cotangent.astype(jnp.float32) * output, axis=-1)
    prob_grad = jnp.einsum("qhv,khv->hqk", cotangent, values, preferred_element_type=jnp.float32)
    score_grad = (
        probability * (prob_grad - jnp.transpose(row_delta)[:, :, None]) * score_scale
    ).astype(jnp.bfloat16)
    nope_query = jnp.einsum(
        "hqk,khd->qhd", score_grad, key_nope, preferred_element_type=jnp.float32
    )
    rope_query = jnp.einsum("hqk,kr->qhr", score_grad, key_rope, preferred_element_type=jnp.float32)
    nope_key = jnp.einsum(
        "hqk,qhd->khd", score_grad, query_nope, preferred_element_type=jnp.float32
    )
    rope_key = jnp.einsum("hqk,qhr->kr", score_grad, query_rope, preferred_element_type=jnp.float32)
    value_grad = jnp.einsum("hqk,qhv->khv", weights, cotangent, preferred_element_type=jnp.float32)
    return (nope_query, rope_query, nope_key, rope_key, value_grad)


def swap_pair(values):
    return lax.ppermute(values, "core", [(0, 1), (1, 0)])


def on_device(queries, latent, prefix, kv_up, out_grad, lengths, positions):
    seq_len = queries.shape[0]
    latent_dim = kv_up.shape[0]
    value_dim = out_grad.shape[2]
    nope_dim = kv_up.shape[2] - value_dim
    rope_dim = latent.shape[1] - latent_dim
    prefix_rows = prefix.shape[0]
    length = lengths[0]
    cosine, sine = angles_of(positions[0], rope_dim)
    query_nope = queries[:, :, :nope_dim]
    query_rope = rotate(
        queries[:, :, nope_dim:].astype(jnp.float32), cosine[:, None], sine[:, None]
    ).astype(jnp.bfloat16)
    token_rope = rotate(latent[:, latent_dim:].astype(jnp.float32), cosine, sine).astype(
        jnp.bfloat16
    )
    source = jnp.concatenate(
        [prefix, jnp.concatenate([latent[:, :latent_dim], token_rope], axis=1)], axis=0
    )
    source_latent = source[:, :latent_dim]
    key_rope = source[:, latent_dim:]
    key_total = source.shape[0]
    live_rows = jnp.arange(seq_len) < length
    cotangent = jnp.where(live_rows[:, None, None], out_grad, jnp.zeros_like(out_grad))
    block_rows = min(seq_len, 256)
    head_part = kv_up.shape[1]
    projected = jnp.einsum(
        "kl,lhd->khd", source_latent, kv_up, preferred_element_type=jnp.float32
    ).astype(jnp.bfloat16)
    key_nope = projected[:, :, :nope_dim]
    values = projected[:, :, nope_dim:]
    nope_total = jnp.zeros((key_total, head_part, nope_dim), jnp.float32)
    rope_total = jnp.zeros((key_total, rope_dim), jnp.float32)
    value_total = jnp.zeros((key_total, head_part, value_dim), jnp.float32)
    query_pieces = []
    for block_number in range(seq_len // block_rows):
        first_row = block_number * block_rows
        last_row = first_row + block_rows
        seen = prefix_rows + last_row
        pieces = block_gradients(
            query_nope[first_row:last_row],
            query_rope[first_row:last_row],
            key_nope[:seen],
            key_rope[:seen],
            values[:seen],
            cotangent[first_row:last_row],
            first_row,
            length,
            prefix_rows,
        )
        nope_query, rope_query, nope_key, rope_key, value_grad = pieces
        nope_total = nope_total.at[:seen].add(nope_key)
        rope_total = rope_total.at[:seen].add(rope_key)
        value_total = value_total.at[:seen].add(value_grad)
        query_pieces.append(
            jnp.concatenate(
                [
                    nope_query,
                    unrotate(
                        rope_query, cosine[first_row:last_row, None], sine[first_row:last_row, None]
                    ),
                ],
                axis=-1,
            ).astype(jnp.bfloat16)
        )
    head_projected_grad = jnp.concatenate([nope_total, value_total], axis=-1).astype(jnp.bfloat16)
    up_part = jnp.einsum(
        "kl,khd->lhd", source_latent, head_projected_grad, preferred_element_type=jnp.float32
    )
    query_grad, projected_grad, rope_grad, up_part = (
        jnp.concatenate(query_pieces, axis=0),
        head_projected_grad,
        rope_total,
        up_part,
    )
    dp_size = lax.axis_size("dp")
    up_pieces = lax.all_to_all(
        up_part.astype(jnp.bfloat16).reshape((dp_size, -1) + up_part.shape[1:]), "dp", 0, 0, tiled=False
    )
    up_grad = jnp.sum(up_pieces.astype(jnp.float32), axis=0)
    token_grad = projected_grad[prefix_rows:]
    token_rope_grad = rope_grad[prefix_rows:]
    latent_part = jnp.einsum("khd,lhd->kl", token_grad, kv_up, preferred_element_type=jnp.float32)
    token_part = jnp.concatenate(
        [latent_part, unrotate(token_rope_grad, cosine, sine)], axis=1
    ).astype(jnp.bfloat16)
    core = lax.axis_index("core")
    pair_size = lax.axis_size("core")
    row_size = lax.axis_size("hr")
    token_blocks = token_part.reshape((row_size, pair_size, -1) + token_part.shape[1:])
    token_mine = jnp.where(core == 0, token_blocks[:, 0], token_blocks[:, 1])
    token_other = jnp.where(core == 0, token_blocks[:, 1], token_blocks[:, 0])
    token_pair = (
        token_mine.astype(jnp.float32) + swap_pair(token_other).astype(jnp.float32)
    ).astype(jnp.bfloat16)
    token_pieces = lax.all_to_all(token_pair, "hr", 0, 0, tiled=False)
    latent_grad = jnp.sum(token_pieces.astype(jnp.float32), axis=0)
    latent_part = jnp.einsum(
        "khd,lhd->kl", projected_grad[:prefix_rows], kv_up, preferred_element_type=jnp.float32
    )
    prefix_part = jnp.concatenate([latent_part, rope_grad[:prefix_rows]], axis=1)
    half_rows = prefix_part.shape[0] // 2
    prefix_mine = lax.dynamic_slice_in_dim(prefix_part, core * half_rows, half_rows)
    prefix_other = lax.dynamic_slice_in_dim(prefix_part, (1 - core) * half_rows, half_rows)
    prefix_half = prefix_mine + swap_pair(prefix_other)
    prefix_rows_part = jnp.sum(
        lax.all_to_all(
            prefix_half.reshape((row_size, -1) + prefix_half.shape[1:]), "hr", 0, 0, tiled=False
        ),
        axis=0,
    )
    prefix_own = jnp.sum(
        lax.all_to_all(
            jnp.broadcast_to(prefix_rows_part[None], (dp_size,) + prefix_rows_part.shape),
            "dp",
            0,
            0,
            tiled=False,
        ),
        axis=0,
    )
    prefix_copies = jnp.broadcast_to(prefix_own[None], (row_size,) + prefix_own.shape)
    prefix_gathered = lax.all_to_all(prefix_copies, "hr", 0, 0, tiled=False).reshape(
        prefix_half.shape
    )
    prefix_partner = swap_pair(prefix_gathered)
    prefix_grad = jnp.where(
        core == 0,
        jnp.concatenate([prefix_gathered, prefix_partner], axis=0),
        jnp.concatenate([prefix_partner, prefix_gathered], axis=0),
    )
    return (query_grad, latent_grad, up_grad, prefix_grad)


def solution(mesh):
    dp_size, head_size = mesh.shape["dp"], mesh.shape["head"]
    split = Mesh(mesh.devices.reshape(dp_size, head_size // 2, 2), ("dp", "hr", "core"))
    head = ("hr", "core")
    placed = (
        P("dp", head, None),
        P("dp", None),
        P(),
        P(None, head, None),
        P("dp", head, None),
        P("dp"),
        P("dp", None),
    )
    return jax.shard_map(
        on_device,
        mesh=split,
        in_specs=placed,
        out_specs=(P("dp", head, None), P(("dp",) + head, None), P("dp", head, None), P()),
        check_vma=False,
    )
```

```python
import jax
import jax.numpy as jnp
from jax import lax
from jax.sharding import Mesh, PartitionSpec as P


def angles_of(positions, rope_dim):
    halfway = rope_dim // 2
    frequency = 10000.0 ** (-(jnp.arange(halfway, dtype=jnp.float32) * 2.0 / rope_dim))
    angles = positions.astype(jnp.float32)[:, None] * frequency[None, :]
    return (jnp.cos(angles), jnp.sin(angles))


def rotate(values, cosine, sine):
    halfway = values.shape[-1] // 2
    leading = values[..., :halfway]
    trailing = values[..., halfway:]
    return jnp.concatenate(
        [leading * cosine - trailing * sine, trailing * cosine + leading * sine], axis=-1
    )


def unrotate(values, cosine, sine):
    halfway = values.shape[-1] // 2
    leading = values[..., :halfway]
    trailing = values[..., halfway:]
    return jnp.concatenate(
        [leading * cosine + trailing * sine, trailing * cosine - leading * sine], axis=-1
    )


def block_gradients(
    query_nope, query_rope, key_nope, key_rope, values, cotangent, first_row, length, prefix_rows
):
    score_scale = (query_nope.shape[-1] + query_rope.shape[-1]) ** (-0.5)
    scores = (
        jnp.einsum("qhd,khd->hqk", query_nope, key_nope, preferred_element_type=jnp.float32)
        + jnp.einsum("qhr,kr->hqk", query_rope, key_rope, preferred_element_type=jnp.float32)
    ) * score_scale
    row_index = first_row + jnp.arange(query_nope.shape[0])
    col_index = jnp.arange(key_nope.shape[0]) - prefix_rows
    allowed = (col_index[None, :] < 0) | (col_index[None, :] <= row_index[:, None]) & (
        col_index[None, :] < length
    )
    scores = jnp.where(allowed[None], scores, -jnp.inf)
    highest = jnp.max(scores, axis=-1, keepdims=True)
    exponent = jnp.exp(scores - highest)
    probability = exponent / jnp.sum(exponent, axis=-1, keepdims=True)
    weights = probability.astype(jnp.bfloat16)
    output = jnp.einsum("hqk,khv->qhv", weights, values, preferred_element_type=jnp.float32)
    row_delta = jnp.sum(cotangent.astype(jnp.float32) * output, axis=-1)
    prob_grad = jnp.einsum("qhv,khv->hqk", cotangent, values, preferred_element_type=jnp.float32)
    score_grad = (
        probability * (prob_grad - jnp.transpose(row_delta)[:, :, None]) * score_scale
    ).astype(jnp.bfloat16)
    nope_query = jnp.einsum(
        "hqk,khd->qhd", score_grad, key_nope, preferred_element_type=jnp.float32
    )
    rope_query = jnp.einsum("hqk,kr->qhr", score_grad, key_rope, preferred_element_type=jnp.float32)
    nope_key = jnp.einsum(
        "hqk,qhd->khd", score_grad, query_nope, preferred_element_type=jnp.float32
    )
    rope_key = jnp.einsum("hqk,qhr->kr", score_grad, query_rope, preferred_element_type=jnp.float32)
    value_grad = jnp.einsum("hqk,qhv->khv", weights, cotangent, preferred_element_type=jnp.float32)
    return (nope_query, rope_query, nope_key, rope_key, value_grad)


def swap_pair(values):
    return lax.ppermute(values, "core", [(0, 1), (1, 0)])


def on_device(queries, latent, prefix, kv_up, out_grad, lengths, positions):
    seq_len = queries.shape[0]
    latent_dim = kv_up.shape[0]
    value_dim = out_grad.shape[2]
    nope_dim = kv_up.shape[2] - value_dim
    rope_dim = latent.shape[1] - latent_dim
    prefix_rows = prefix.shape[0]
    length = lengths[0]
    cosine, sine = angles_of(positions[0], rope_dim)
    query_nope = queries[:, :, :nope_dim]
    query_rope = rotate(
        queries[:, :, nope_dim:].astype(jnp.float32), cosine[:, None], sine[:, None]
    ).astype(jnp.bfloat16)
    token_rope = rotate(latent[:, latent_dim:].astype(jnp.float32), cosine, sine).astype(
        jnp.bfloat16
    )
    source = jnp.concatenate(
        [prefix, jnp.concatenate([latent[:, :latent_dim], token_rope], axis=1)], axis=0
    )
    source_latent = source[:, :latent_dim]
    key_rope = source[:, latent_dim:]
    key_total = source.shape[0]
    live_rows = jnp.arange(seq_len) < length
    cotangent = jnp.where(live_rows[:, None, None], out_grad, jnp.zeros_like(out_grad))
    block_rows = min(seq_len, 256)
    head_part = kv_up.shape[1]
    projected = jnp.einsum(
        "kl,lhd->khd", source_latent, kv_up, preferred_element_type=jnp.float32
    ).astype(jnp.bfloat16)
    key_nope = projected[:, :, :nope_dim]
    values = projected[:, :, nope_dim:]
    nope_total = jnp.zeros((key_total, head_part, nope_dim), jnp.float32)
    rope_total = jnp.zeros((key_total, rope_dim), jnp.float32)
    value_total = jnp.zeros((key_total, head_part, value_dim), jnp.float32)
    query_pieces = []
    for block_number in range(seq_len // block_rows):
        first_row = block_number * block_rows
        last_row = first_row + block_rows
        seen = prefix_rows + last_row
        pieces = block_gradients(
            query_nope[first_row:last_row],
            query_rope[first_row:last_row],
            key_nope[:seen],
            key_rope[:seen],
            values[:seen],
            cotangent[first_row:last_row],
            first_row,
            length,
            prefix_rows,
        )
        nope_query, rope_query, nope_key, rope_key, value_grad = pieces
        nope_total = nope_total.at[:seen].add(nope_key)
        rope_total = rope_total.at[:seen].add(rope_key)
        value_total = value_total.at[:seen].add(value_grad)
        query_pieces.append(
            jnp.concatenate(
                [
                    nope_query,
                    unrotate(
                        rope_query, cosine[first_row:last_row, None], sine[first_row:last_row, None]
                    ),
                ],
                axis=-1,
            ).astype(jnp.bfloat16)
        )
    head_projected_grad = jnp.concatenate([nope_total, value_total], axis=-1).astype(jnp.bfloat16)
    up_part = jnp.einsum(
        "kl,khd->lhd", source_latent, head_projected_grad, preferred_element_type=jnp.float32
    )
    query_grad, projected_grad, rope_grad, up_part = (
        jnp.concatenate(query_pieces, axis=0),
        head_projected_grad,
        rope_total,
        up_part,
    )
    dp_size = lax.axis_size("dp")
    up_pieces = lax.all_to_all(
        up_part.astype(jnp.bfloat16).reshape((dp_size, -1) + up_part.shape[1:]), "dp", 0, 0, tiled=False
    )
    up_grad = jnp.sum(up_pieces.astype(jnp.float32), axis=0)
    token_grad = projected_grad[prefix_rows:]
    token_rope_grad = rope_grad[prefix_rows:]
    latent_part = jnp.einsum("khd,lhd->kl", token_grad, kv_up, preferred_element_type=jnp.float32)
    token_part = jnp.concatenate(
        [latent_part, unrotate(token_rope_grad, cosine, sine)], axis=1
    ).astype(jnp.bfloat16)
    core = lax.axis_index("core")
    pair_size = lax.axis_size("core")
    row_size = lax.axis_size("hr")
    token_blocks = token_part.reshape((row_size, pair_size, -1) + token_part.shape[1:])
    token_mine = jnp.where(core == 0, token_blocks[:, 0], token_blocks[:, 1])
    token_other = jnp.where(core == 0, token_blocks[:, 1], token_blocks[:, 0])
    token_pair = (
        token_mine.astype(jnp.float32) + swap_pair(token_other).astype(jnp.float32)
    ).astype(jnp.bfloat16)
    token_pieces = lax.all_to_all(token_pair, "hr", 0, 0, tiled=False)
    latent_grad = jnp.sum(token_pieces.astype(jnp.float32), axis=0)
    latent_part = jnp.einsum(
        "khd,lhd->kl", projected_grad[:prefix_rows], kv_up, preferred_element_type=jnp.float32
    )
    prefix_part = jnp.concatenate([latent_part, rope_grad[:prefix_rows]], axis=1)
    half_rows = prefix_part.shape[0] // 2
    prefix_mine = lax.dynamic_slice_in_dim(prefix_part, core * half_rows, half_rows)
    prefix_other = lax.dynamic_slice_in_dim(prefix_part, (1 - core) * half_rows, half_rows)
    prefix_half = prefix_mine + swap_pair(prefix_other)
    prefix_rows_part = jnp.sum(
        lax.all_to_all(
            prefix_half.reshape((row_size, -1) + prefix_half.shape[1:]), "hr", 0, 0, tiled=False
        ),
        axis=0,
    )
    prefix_own = prefix_rows_part
    stride = 1
    while stride < dp_size:
        partners = [(i, i ^ stride) for i in range(dp_size)]
        prefix_own = prefix_own + lax.ppermute(prefix_own, "dp", partners)
        stride *= 2
    prefix_copies = jnp.broadcast_to(prefix_own[None], (row_size,) + prefix_own.shape)
    prefix_gathered = lax.all_to_all(prefix_copies, "hr", 0, 0, tiled=False).reshape(
        prefix_half.shape
    )
    prefix_partner = swap_pair(prefix_gathered)
    prefix_grad = jnp.where(
        core == 0,
        jnp.concatenate([prefix_gathered, prefix_partner], axis=0),
        jnp.concatenate([prefix_partner, prefix_gathered], axis=0),
    )
    return (query_grad, latent_grad, up_grad, prefix_grad)


def solution(mesh):
    dp_size, head_size = mesh.shape["dp"], mesh.shape["head"]
    split = Mesh(mesh.devices.reshape(dp_size, head_size // 2, 2), ("dp", "hr", "core"))
    head = ("hr", "core")
    placed = (
        P("dp", head, None),
        P("dp", None),
        P(),
        P(None, head, None),
        P("dp", head, None),
        P("dp"),
        P("dp", None),
    )
    return jax.shard_map(
        on_device,
        mesh=split,
        in_specs=placed,
        out_specs=(P("dp", head, None), P(("dp",) + head, None), P("dp", head, None), P()),
        check_vma=False,
    )
```

```python
import jax
import jax.numpy as jnp
from jax import lax
from jax.sharding import Mesh, PartitionSpec as P


def angles_of(positions, rope_dim):
    halfway = rope_dim // 2
    frequency = 10000.0 ** (-(jnp.arange(halfway, dtype=jnp.float32) * 2.0 / rope_dim))
    angles = positions.astype(jnp.float32)[:, None] * frequency[None, :]
    return (jnp.cos(angles), jnp.sin(angles))


def rotate(values, cosine, sine):
    halfway = values.shape[-1] // 2
    leading = values[..., :halfway]
    trailing = values[..., halfway:]
    return jnp.concatenate(
        [leading * cosine - trailing * sine, trailing * cosine + leading * sine], axis=-1
    )


def unrotate(values, cosine, sine):
    halfway = values.shape[-1] // 2
    leading = values[..., :halfway]
    trailing = values[..., halfway:]
    return jnp.concatenate(
        [leading * cosine + trailing * sine, trailing * cosine - leading * sine], axis=-1
    )


def block_gradients(query_used, key_used, values, cotangent, first_row, length, prefix_rows):
    nope_dim = values.shape[-1]
    score_scale = query_used.shape[-1] ** (-0.5)
    scores = (
        jnp.einsum("qhd,khd->hqk", query_used, key_used, preferred_element_type=jnp.float32)
        * score_scale
    )
    row_index = first_row + jnp.arange(query_used.shape[0])
    col_index = jnp.arange(key_used.shape[0]) - prefix_rows
    allowed = (col_index[None, :] < 0) | (col_index[None, :] <= row_index[:, None]) & (
        col_index[None, :] < length
    )
    scores = jnp.where(allowed[None], scores, -jnp.inf)
    highest = jnp.max(scores, axis=-1, keepdims=True)
    exponent = jnp.exp(scores - highest)
    probability = exponent / jnp.sum(exponent, axis=-1, keepdims=True)
    weights = probability.astype(jnp.bfloat16)
    output = jnp.einsum("hqk,khv->qhv", weights, values, preferred_element_type=jnp.float32)
    row_delta = jnp.sum(cotangent.astype(jnp.float32) * output, axis=-1)
    prob_grad = jnp.einsum("qhv,khv->hqk", cotangent, values, preferred_element_type=jnp.float32)
    score_grad = (
        probability * (prob_grad - jnp.transpose(row_delta)[:, :, None]) * score_scale
    ).astype(jnp.bfloat16)
    query_part = jnp.einsum("hqk,khd->qhd", score_grad, key_used, preferred_element_type=jnp.float32)
    key_part = jnp.einsum("hqk,qhd->khd", score_grad, query_used, preferred_element_type=jnp.float32)
    nope_query = query_part[:, :, :nope_dim]
    rope_query = query_part[:, :, nope_dim:]
    nope_key = key_part[:, :, :nope_dim]
    rope_key = jnp.sum(key_part[:, :, nope_dim:], axis=1)
    value_grad = jnp.einsum("hqk,qhv->khv", weights, cotangent, preferred_element_type=jnp.float32)
    return (nope_query, rope_query, nope_key, rope_key, value_grad)


def swap_pair(values):
    return lax.ppermute(values, "core", [(0, 1), (1, 0)])


def on_device(queries, latent, prefix, kv_up, out_grad, lengths, positions):
    seq_len = queries.shape[0]
    latent_dim = kv_up.shape[0]
    value_dim = out_grad.shape[2]
    nope_dim = kv_up.shape[2] - value_dim
    rope_dim = latent.shape[1] - latent_dim
    prefix_rows = prefix.shape[0]
    length = lengths[0]
    cosine, sine = angles_of(positions[0], rope_dim)
    query_nope = queries[:, :, :nope_dim]
    query_rope = rotate(
        queries[:, :, nope_dim:].astype(jnp.float32), cosine[:, None], sine[:, None]
    ).astype(jnp.bfloat16)
    token_rope = rotate(latent[:, latent_dim:].astype(jnp.float32), cosine, sine).astype(
        jnp.bfloat16
    )
    source = jnp.concatenate(
        [prefix, jnp.concatenate([latent[:, :latent_dim], token_rope], axis=1)], axis=0
    )
    source_latent = source[:, :latent_dim]
    key_rope = source[:, latent_dim:]
    key_total = source.shape[0]
    live_rows = jnp.arange(seq_len) < length
    cotangent = jnp.where(live_rows[:, None, None], out_grad, jnp.zeros_like(out_grad))
    block_rows = min(seq_len, 256)
    head_part = kv_up.shape[1]
    projected = jnp.einsum(
        "kl,lhd->khd", source_latent, kv_up, preferred_element_type=jnp.float32
    ).astype(jnp.bfloat16)
    key_nope = projected[:, :, :nope_dim]
    values = projected[:, :, nope_dim:]
    query_used = jnp.concatenate([query_nope, query_rope], axis=-1)
    key_used = jnp.concatenate(
        [key_nope, jnp.broadcast_to(key_rope[:, None, :], key_rope.shape[:1] + (head_part,) + key_rope.shape[1:])],
        axis=-1,
    )
    nope_total = jnp.zeros((key_total, head_part, nope_dim), jnp.float32)
    rope_total = jnp.zeros((key_total, rope_dim), jnp.float32)
    value_total = jnp.zeros((key_total, head_part, value_dim), jnp.float32)
    query_pieces = []
    for block_number in range(seq_len // block_rows):
        first_row = block_number * block_rows
        last_row = first_row + block_rows
        seen = prefix_rows + last_row
        pieces = block_gradients(
            query_used[first_row:last_row],
            key_used[:seen],
            values[:seen],
            cotangent[first_row:last_row],
            first_row,
            length,
            prefix_rows,
        )
        nope_query, rope_query, nope_key, rope_key, value_grad = pieces
        nope_total = nope_total.at[:seen].add(nope_key)
        rope_total = rope_total.at[:seen].add(rope_key)
        value_total = value_total.at[:seen].add(value_grad)
        query_pieces.append(
            jnp.concatenate(
                [
                    nope_query,
                    unrotate(
                        rope_query, cosine[first_row:last_row, None], sine[first_row:last_row, None]
                    ),
                ],
                axis=-1,
            ).astype(jnp.bfloat16)
        )
    head_projected_grad = jnp.concatenate([nope_total, value_total], axis=-1).astype(jnp.bfloat16)
    up_part = jnp.einsum(
        "kl,khd->lhd", source_latent, head_projected_grad, preferred_element_type=jnp.float32
    )
    query_grad, projected_grad, rope_grad, up_part = (
        jnp.concatenate(query_pieces, axis=0),
        head_projected_grad,
        rope_total,
        up_part,
    )
    dp_size = lax.axis_size("dp")
    up_pieces = lax.all_to_all(
        up_part.astype(jnp.bfloat16).reshape((dp_size, -1) + up_part.shape[1:]), "dp", 0, 0, tiled=False
    )
    up_grad = jnp.sum(up_pieces.astype(jnp.float32), axis=0)
    token_grad = projected_grad[prefix_rows:]
    token_rope_grad = rope_grad[prefix_rows:]
    latent_part = jnp.einsum("khd,lhd->kl", token_grad, kv_up, preferred_element_type=jnp.float32)
    token_part = jnp.concatenate(
        [latent_part, unrotate(token_rope_grad, cosine, sine)], axis=1
    ).astype(jnp.bfloat16)
    core = lax.axis_index("core")
    pair_size = lax.axis_size("core")
    row_size = lax.axis_size("hr")
    token_blocks = token_part.reshape((row_size, pair_size, -1) + token_part.shape[1:])
    token_mine = jnp.where(core == 0, token_blocks[:, 0], token_blocks[:, 1])
    token_other = jnp.where(core == 0, token_blocks[:, 1], token_blocks[:, 0])
    token_pair = (
        token_mine.astype(jnp.float32) + swap_pair(token_other).astype(jnp.float32)
    ).astype(jnp.bfloat16)
    token_pieces = lax.all_to_all(token_pair, "hr", 0, 0, tiled=False)
    latent_grad = jnp.sum(token_pieces.astype(jnp.float32), axis=0)
    latent_part = jnp.einsum(
        "khd,lhd->kl", projected_grad[:prefix_rows], kv_up, preferred_element_type=jnp.float32
    )
    prefix_part = jnp.concatenate([latent_part, rope_grad[:prefix_rows]], axis=1)
    half_rows = prefix_part.shape[0] // 2
    prefix_mine = lax.dynamic_slice_in_dim(prefix_part, core * half_rows, half_rows)
    prefix_other = lax.dynamic_slice_in_dim(prefix_part, (1 - core) * half_rows, half_rows)
    prefix_half = prefix_mine + swap_pair(prefix_other)
    prefix_rows_part = jnp.sum(
        lax.all_to_all(
            prefix_half.reshape((row_size, -1) + prefix_half.shape[1:]), "hr", 0, 0, tiled=False
        ),
        axis=0,
    )
    prefix_own = prefix_rows_part
    stride = 1
    while stride < dp_size:
        partners = [(i, i ^ stride) for i in range(dp_size)]
        prefix_own = prefix_own + lax.ppermute(prefix_own, "dp", partners)
        stride *= 2
    prefix_copies = jnp.broadcast_to(prefix_own[None], (row_size,) + prefix_own.shape)
    prefix_gathered = lax.all_to_all(prefix_copies, "hr", 0, 0, tiled=False).reshape(
        prefix_half.shape
    )
    prefix_partner = swap_pair(prefix_gathered)
    prefix_grad = jnp.where(
        core == 0,
        jnp.concatenate([prefix_gathered, prefix_partner], axis=0),
        jnp.concatenate([prefix_partner, prefix_gathered], axis=0),
    )
    return (query_grad, latent_grad, up_grad, prefix_grad)


def solution(mesh):
    dp_size, head_size = mesh.shape["dp"], mesh.shape["head"]
    split = Mesh(mesh.devices.reshape(dp_size, head_size // 2, 2), ("dp", "hr", "core"))
    head = ("hr", "core")
    placed = (
        P("dp", head, None),
        P("dp", None),
        P(),
        P(None, head, None),
        P("dp", head, None),
        P("dp"),
        P("dp", None),
    )
    return jax.shard_map(
        on_device,
        mesh=split,
        in_specs=placed,
        out_specs=(P("dp", head, None), P(("dp",) + head, None), P("dp", head, None), P()),
        check_vma=False,
    )
```

```python
import jax
import jax.numpy as jnp
from jax import lax
from jax.sharding import Mesh, PartitionSpec as P


def angles_of(positions, rope_dim):
    halfway = rope_dim // 2
    frequency = 10000.0 ** (-(jnp.arange(halfway, dtype=jnp.float32) * 2.0 / rope_dim))
    angles = positions.astype(jnp.float32)[:, None] * frequency[None, :]
    return (jnp.cos(angles), jnp.sin(angles))


def rotate(values, cosine, sine):
    halfway = values.shape[-1] // 2
    leading = values[..., :halfway]
    trailing = values[..., halfway:]
    return jnp.concatenate(
        [leading * cosine - trailing * sine, trailing * cosine + leading * sine], axis=-1
    )


def unrotate(values, cosine, sine):
    halfway = values.shape[-1] // 2
    leading = values[..., :halfway]
    trailing = values[..., halfway:]
    return jnp.concatenate(
        [leading * cosine + trailing * sine, trailing * cosine - leading * sine], axis=-1
    )


def block_gradients(query_used, key_used, values, cotangent, first_row, length, prefix_rows):
    nope_dim = values.shape[-1]
    score_scale = query_used.shape[-1] ** (-0.5)
    scores = (
        jnp.einsum("qhd,khd->hqk", query_used, key_used, preferred_element_type=jnp.float32)
        * score_scale
    )
    row_index = first_row + jnp.arange(query_used.shape[0])
    col_index = jnp.arange(key_used.shape[0]) - prefix_rows
    allowed = (col_index[None, :] < 0) | (col_index[None, :] <= row_index[:, None]) & (
        col_index[None, :] < length
    )
    scores = jnp.where(allowed[None], scores, -jnp.inf)
    highest = jnp.max(scores, axis=-1, keepdims=True)
    exponent = jnp.exp(scores - highest)
    probability = exponent / jnp.sum(exponent, axis=-1, keepdims=True)
    weights = probability.astype(jnp.bfloat16)
    output = jnp.einsum("hqk,khv->qhv", weights, values, preferred_element_type=jnp.float32)
    row_delta = jnp.sum(cotangent.astype(jnp.float32) * output, axis=-1)
    prob_grad = jnp.einsum("qhv,khv->hqk", cotangent, values, preferred_element_type=jnp.float32)
    score_grad = (
        probability * (prob_grad - jnp.transpose(row_delta)[:, :, None]) * score_scale
    ).astype(jnp.bfloat16)
    query_part = jnp.einsum("hqk,khd->qhd", score_grad, key_used, preferred_element_type=jnp.float32)
    key_part = jnp.einsum("hqk,qhd->khd", score_grad, query_used, preferred_element_type=jnp.float32)
    nope_query = query_part[:, :, :nope_dim]
    rope_query = query_part[:, :, nope_dim:]
    nope_key = key_part[:, :, :nope_dim]
    rope_key = jnp.sum(key_part[:, :, nope_dim:], axis=1)
    value_grad = jnp.einsum("hqk,qhv->khv", weights, cotangent, preferred_element_type=jnp.float32)
    return (nope_query, rope_query, nope_key, rope_key, value_grad)


def swap_pair(values):
    return lax.ppermute(values, "core", [(0, 1), (1, 0)])


def device_step(queries, latent, prefix, kv_up, out_grad, lengths, positions):
    seq_len = queries.shape[0]
    latent_dim = kv_up.shape[0]
    value_dim = out_grad.shape[2]
    nope_dim = kv_up.shape[2] - value_dim
    rope_dim = latent.shape[1] - latent_dim
    prefix_rows = prefix.shape[0]
    length = lengths[0]
    cosine, sine = angles_of(positions[0], rope_dim)
    query_nope = queries[:, :, :nope_dim]
    query_rope = rotate(
        queries[:, :, nope_dim:].astype(jnp.float32), cosine[:, None], sine[:, None]
    ).astype(jnp.bfloat16)
    token_rope = rotate(latent[:, latent_dim:].astype(jnp.float32), cosine, sine).astype(
        jnp.bfloat16
    )
    source = jnp.concatenate(
        [prefix, jnp.concatenate([latent[:, :latent_dim], token_rope], axis=1)], axis=0
    )
    source_latent = source[:, :latent_dim]
    key_rope = source[:, latent_dim:]
    key_total = source.shape[0]
    live_rows = jnp.arange(seq_len) < length
    cotangent = jnp.where(live_rows[:, None, None], out_grad, jnp.zeros_like(out_grad))
    block_rows = min(seq_len, 256)
    head_part = kv_up.shape[1]
    projected = jnp.einsum(
        "kl,lhd->khd", source_latent, kv_up, preferred_element_type=jnp.float32
    ).astype(jnp.bfloat16)
    key_nope = projected[:, :, :nope_dim]
    values = projected[:, :, nope_dim:]
    query_used = jnp.concatenate([query_nope, query_rope], axis=-1)
    key_used = jnp.concatenate(
        [key_nope, jnp.broadcast_to(key_rope[:, None, :], key_rope.shape[:1] + (head_part,) + key_rope.shape[1:])],
        axis=-1,
    )
    nope_total = jnp.zeros((key_total, head_part, nope_dim), jnp.float32)
    rope_total = jnp.zeros((key_total, rope_dim), jnp.float32)
    value_total = jnp.zeros((key_total, head_part, value_dim), jnp.float32)
    query_pieces = []
    for block_number in range(seq_len // block_rows):
        first_row = block_number * block_rows
        last_row = first_row + block_rows
        seen = prefix_rows + last_row
        pieces = block_gradients(
            query_used[first_row:last_row],
            key_used[:seen],
            values[:seen],
            cotangent[first_row:last_row],
            first_row,
            length,
            prefix_rows,
        )
        nope_query, rope_query, nope_key, rope_key, value_grad = pieces
        nope_total = nope_total.at[:seen].add(nope_key)
        rope_total = rope_total.at[:seen].add(rope_key)
        value_total = value_total.at[:seen].add(value_grad)
        query_pieces.append(
            jnp.concatenate(
                [
                    nope_query,
                    unrotate(
                        rope_query, cosine[first_row:last_row, None], sine[first_row:last_row, None]
                    ),
                ],
                axis=-1,
            ).astype(jnp.bfloat16)
        )
    head_projected_grad = jnp.concatenate([nope_total, value_total], axis=-1).astype(jnp.bfloat16)
    up_part = jnp.einsum(
        "kl,khd->lhd", source_latent, head_projected_grad, preferred_element_type=jnp.float32
    )
    query_grad, projected_grad, rope_grad, up_part = (
        jnp.concatenate(query_pieces, axis=0),
        head_projected_grad,
        rope_total,
        up_part,
    )
    dp_size = lax.axis_size("dp")
    up_pieces = lax.all_to_all(
        up_part.astype(jnp.bfloat16).reshape((dp_size, -1) + up_part.shape[1:]),
        "dp",
        0,
        0,
        tiled=False,
    )
    up_grad = jnp.sum(up_pieces.astype(jnp.float32), axis=0)
    token_grad = projected_grad[prefix_rows:]
    token_rope_grad = rope_grad[prefix_rows:]
    latent_part = jnp.einsum("khd,lhd->kl", token_grad, kv_up, preferred_element_type=jnp.float32)
    token_part = jnp.concatenate(
        [latent_part, unrotate(token_rope_grad, cosine, sine)], axis=1
    ).astype(jnp.bfloat16)
    core = lax.axis_index("core")
    pair_size = lax.axis_size("core")
    row_size = lax.axis_size("hr")
    token_blocks = token_part.reshape((row_size, pair_size, -1) + token_part.shape[1:])
    token_mine = jnp.where(core == 0, token_blocks[:, 0], token_blocks[:, 1])
    token_other = jnp.where(core == 0, token_blocks[:, 1], token_blocks[:, 0])
    token_pair = (
        token_mine.astype(jnp.float32) + swap_pair(token_other).astype(jnp.float32)
    ).astype(jnp.bfloat16)
    token_pieces = lax.all_to_all(token_pair, "hr", 0, 0, tiled=False)
    latent_grad = jnp.sum(token_pieces.astype(jnp.float32), axis=0)
    latent_part = jnp.einsum(
        "khd,lhd->kl", projected_grad[:prefix_rows], kv_up, preferred_element_type=jnp.float32
    )
    prefix_part = jnp.concatenate([latent_part, rope_grad[:prefix_rows]], axis=1)
    half_rows = prefix_part.shape[0] // 2
    prefix_mine = lax.dynamic_slice_in_dim(prefix_part, core * half_rows, half_rows)
    prefix_other = lax.dynamic_slice_in_dim(prefix_part, (1 - core) * half_rows, half_rows)
    prefix_half = prefix_mine + swap_pair(prefix_other)
    prefix_rows_part = jnp.sum(
        lax.all_to_all(
            prefix_half.reshape((row_size, -1) + prefix_half.shape[1:]), "hr", 0, 0, tiled=False
        ),
        axis=0,
    )
    prefix_own = prefix_rows_part
    stride = 1
    while stride < dp_size:
        partners = [(i, i ^ stride) for i in range(dp_size)]
        prefix_own = prefix_own + lax.ppermute(prefix_own, "dp", partners)
        stride *= 2
    prefix_copies = jnp.broadcast_to(prefix_own[None], (row_size,) + prefix_own.shape)
    prefix_gathered = lax.all_to_all(prefix_copies, "hr", 0, 0, tiled=False).reshape(
        prefix_half.shape
    )
    prefix_partner = swap_pair(prefix_gathered)
    prefix_grad = jnp.where(
        core == 0,
        jnp.concatenate([prefix_gathered, prefix_partner], axis=0),
        jnp.concatenate([prefix_partner, prefix_gathered], axis=0),
    )
    return (query_grad, latent_grad, up_grad, prefix_grad)


def solution(mesh):
    dp_size, head_size = mesh.shape["dp"], mesh.shape["head"]
    split = Mesh(mesh.devices.reshape(dp_size, head_size // 2, 2), ("dp", "hr", "core"))
    head = ("hr", "core")
    placed = (
        P("dp", head, None),
        P("dp", None),
        P(),
        P(None, head, None),
        P("dp", head, None),
        P("dp"),
        P("dp", None),
    )
    return jax.shard_map(
        device_step,
        mesh=split,
        in_specs=placed,
        out_specs=(P("dp", head, None), P(("dp",) + head, None), P("dp", head, None), P()),
        check_vma=False,
    )
```

```python
import jax
import jax.numpy as jnp
from jax import lax
from jax.sharding import Mesh, PartitionSpec as P


def angles_of(positions, rope_dim):
    halfway = rope_dim // 2
    frequency = 10000.0 ** (-(jnp.arange(halfway, dtype=jnp.float32) * 2.0 / rope_dim))
    angles = positions.astype(jnp.float32)[:, None] * frequency[None, :]
    return (jnp.cos(angles), jnp.sin(angles))


def rotate(values, cosine, sine):
    halfway = values.shape[-1] // 2
    leading = values[..., :halfway]
    trailing = values[..., halfway:]
    return jnp.concatenate(
        [leading * cosine - trailing * sine, trailing * cosine + leading * sine], axis=-1
    )


def unrotate(values, cosine, sine):
    halfway = values.shape[-1] // 2
    leading = values[..., :halfway]
    trailing = values[..., halfway:]
    return jnp.concatenate(
        [leading * cosine + trailing * sine, trailing * cosine - leading * sine], axis=-1
    )


def block_gradients(query_used, key_used, values, cotangent, first_row, length, prefix_rows):
    nope_dim = values.shape[-1]
    score_scale = query_used.shape[-1] ** (-0.5)
    scores = (
        jnp.einsum("qhd,khd->hqk", query_used, key_used, preferred_element_type=jnp.float32)
        * score_scale
    )
    row_index = first_row + jnp.arange(query_used.shape[0])
    col_index = jnp.arange(key_used.shape[0]) - prefix_rows
    allowed = (col_index[None, :] < 0) | (col_index[None, :] <= row_index[:, None]) & (
        col_index[None, :] < length
    )
    scores = jnp.where(allowed[None], scores, -jnp.inf)
    highest = jnp.max(scores, axis=-1, keepdims=True)
    exponent = jnp.exp(scores - highest)
    probability = exponent / jnp.sum(exponent, axis=-1, keepdims=True)
    weights = probability.astype(jnp.bfloat16)
    output = jnp.einsum("hqk,khv->qhv", weights, values, preferred_element_type=jnp.float32)
    row_delta = jnp.sum(cotangent.astype(jnp.float32) * output, axis=-1)
    prob_grad = jnp.einsum("qhv,khv->hqk", cotangent, values, preferred_element_type=jnp.float32)
    score_grad = (
        probability * (prob_grad - jnp.transpose(row_delta)[:, :, None]) * score_scale
    ).astype(jnp.bfloat16)
    query_part = jnp.einsum("hqk,khd->qhd", score_grad, key_used, preferred_element_type=jnp.float32)
    key_part = jnp.einsum("hqk,qhd->khd", score_grad, query_used, preferred_element_type=jnp.float32)
    nope_query = query_part[:, :, :nope_dim]
    rope_query = query_part[:, :, nope_dim:]
    nope_key = key_part[:, :, :nope_dim]
    rope_key = jnp.sum(key_part[:, :, nope_dim:], axis=1)
    value_grad = jnp.einsum("hqk,qhv->khv", weights, cotangent, preferred_element_type=jnp.float32)
    return (nope_query, rope_query, nope_key, rope_key, value_grad)


def swap_pair(values):
    return lax.ppermute(values, "core", [(0, 1), (1, 0)])


def on_device(queries, latent, prefix, kv_up, out_grad, lengths, positions):
    seq_len = queries.shape[0]
    latent_dim = kv_up.shape[0]
    value_dim = out_grad.shape[2]
    nope_dim = kv_up.shape[2] - value_dim
    rope_dim = latent.shape[1] - latent_dim
    prefix_rows = prefix.shape[0]
    length = lengths[0]
    cosine, sine = angles_of(positions[0], rope_dim)
    query_nope = queries[:, :, :nope_dim]
    query_rope = rotate(
        queries[:, :, nope_dim:].astype(jnp.float32), cosine[:, None], sine[:, None]
    ).astype(jnp.bfloat16)
    token_rope = rotate(latent[:, latent_dim:].astype(jnp.float32), cosine, sine).astype(
        jnp.bfloat16
    )
    source = jnp.concatenate(
        [prefix, jnp.concatenate([latent[:, :latent_dim], token_rope], axis=1)], axis=0
    )
    source_latent = source[:, :latent_dim]
    key_rope = source[:, latent_dim:]
    key_total = source.shape[0]
    live_rows = jnp.arange(seq_len) < length
    cotangent = jnp.where(live_rows[:, None, None], out_grad, jnp.zeros_like(out_grad))
    block_rows = seq_len
    head_part = kv_up.shape[1]
    projected = jnp.einsum(
        "kl,lhd->khd", source_latent, kv_up, preferred_element_type=jnp.float32
    ).astype(jnp.bfloat16)
    key_nope = projected[:, :, :nope_dim]
    values = projected[:, :, nope_dim:]
    query_used = jnp.concatenate([query_nope, query_rope], axis=-1)
    key_used = jnp.concatenate(
        [key_nope, jnp.broadcast_to(key_rope[:, None, :], key_rope.shape[:1] + (head_part,) + key_rope.shape[1:])],
        axis=-1,
    )
    nope_total = jnp.zeros((key_total, head_part, nope_dim), jnp.float32)
    rope_total = jnp.zeros((key_total, rope_dim), jnp.float32)
    value_total = jnp.zeros((key_total, head_part, value_dim), jnp.float32)
    query_pieces = []
    for block_number in range(seq_len // block_rows):
        first_row = block_number * block_rows
        last_row = first_row + block_rows
        seen = prefix_rows + last_row
        pieces = block_gradients(
            query_used[first_row:last_row],
            key_used[:seen],
            values[:seen],
            cotangent[first_row:last_row],
            first_row,
            length,
            prefix_rows,
        )
        nope_query, rope_query, nope_key, rope_key, value_grad = pieces
        nope_total = nope_total.at[:seen].add(nope_key)
        rope_total = rope_total.at[:seen].add(rope_key)
        value_total = value_total.at[:seen].add(value_grad)
        query_pieces.append(
            jnp.concatenate(
                [
                    nope_query,
                    unrotate(
                        rope_query, cosine[first_row:last_row, None], sine[first_row:last_row, None]
                    ),
                ],
                axis=-1,
            ).astype(jnp.bfloat16)
        )
    head_projected_grad = jnp.concatenate([nope_total, value_total], axis=-1).astype(jnp.bfloat16)
    up_part = jnp.einsum(
        "kl,khd->lhd", source_latent, head_projected_grad, preferred_element_type=jnp.float32
    )
    query_grad, projected_grad, rope_grad, up_part = (
        jnp.concatenate(query_pieces, axis=0),
        head_projected_grad,
        rope_total,
        up_part,
    )
    dp_size = lax.axis_size("dp")
    up_pieces = lax.all_to_all(
        up_part.astype(jnp.bfloat16).reshape((dp_size, -1) + up_part.shape[1:]), "dp", 0, 0, tiled=False
    )
    up_grad = jnp.sum(up_pieces.astype(jnp.float32), axis=0)
    token_grad = projected_grad[prefix_rows:]
    token_rope_grad = rope_grad[prefix_rows:]
    latent_part = jnp.einsum("khd,lhd->kl", token_grad, kv_up, preferred_element_type=jnp.float32)
    token_part = jnp.concatenate(
        [latent_part, unrotate(token_rope_grad, cosine, sine)], axis=1
    ).astype(jnp.bfloat16)
    core = lax.axis_index("core")
    pair_size = lax.axis_size("core")
    row_size = lax.axis_size("hr")
    token_blocks = token_part.reshape((row_size, pair_size, -1) + token_part.shape[1:])
    token_mine = jnp.where(core == 0, token_blocks[:, 0], token_blocks[:, 1])
    token_other = jnp.where(core == 0, token_blocks[:, 1], token_blocks[:, 0])
    token_pair = (
        token_mine.astype(jnp.float32) + swap_pair(token_other).astype(jnp.float32)
    ).astype(jnp.bfloat16)
    token_pieces = lax.all_to_all(token_pair, "hr", 0, 0, tiled=False)
    latent_grad = jnp.sum(token_pieces.astype(jnp.float32), axis=0)
    latent_part = jnp.einsum(
        "khd,lhd->kl", projected_grad[:prefix_rows], kv_up, preferred_element_type=jnp.float32
    )
    prefix_part = jnp.concatenate([latent_part, rope_grad[:prefix_rows]], axis=1)
    half_rows = prefix_part.shape[0] // 2
    prefix_mine = lax.dynamic_slice_in_dim(prefix_part, core * half_rows, half_rows)
    prefix_other = lax.dynamic_slice_in_dim(prefix_part, (1 - core) * half_rows, half_rows)
    prefix_half = prefix_mine + swap_pair(prefix_other)
    prefix_rows_part = jnp.sum(
        lax.all_to_all(
            prefix_half.reshape((row_size, -1) + prefix_half.shape[1:]), "hr", 0, 0, tiled=False
        ),
        axis=0,
    )
    prefix_own = prefix_rows_part
    stride = 1
    while stride < dp_size:
        partners = [(i, i ^ stride) for i in range(dp_size)]
        prefix_own = prefix_own + lax.ppermute(prefix_own, "dp", partners)
        stride *= 2
    prefix_copies = jnp.broadcast_to(prefix_own[None], (row_size,) + prefix_own.shape)
    prefix_gathered = lax.all_to_all(prefix_copies, "hr", 0, 0, tiled=False).reshape(
        prefix_half.shape
    )
    prefix_partner = swap_pair(prefix_gathered)
    prefix_grad = jnp.where(
        core == 0,
        jnp.concatenate([prefix_gathered, prefix_partner], axis=0),
        jnp.concatenate([prefix_partner, prefix_gathered], axis=0),
    )
    return (query_grad, latent_grad, up_grad, prefix_grad)


def solution(mesh):
    dp_size, head_size = mesh.shape["dp"], mesh.shape["head"]
    split = Mesh(mesh.devices.reshape(dp_size, head_size // 2, 2), ("dp", "hr", "core"))
    head = ("hr", "core")
    placed = (
        P("dp", head, None),
        P("dp", None),
        P(),
        P(None, head, None),
        P("dp", head, None),
        P("dp"),
        P("dp", None),
    )
    return jax.shard_map(
        on_device,
        mesh=split,
        in_specs=placed,
        out_specs=(P("dp", head, None), P(("dp",) + head, None), P("dp", head, None), P()),
        check_vma=False,
    )
```

```python
import jax
import jax.numpy as jnp
from jax import lax
from jax.sharding import Mesh, PartitionSpec as P


def angles_of(positions, rope_dim):
    halfway = rope_dim // 2
    frequency = 10000.0 ** (-(jnp.arange(halfway, dtype=jnp.float32) * 2.0 / rope_dim))
    angles = positions.astype(jnp.float32)[:, None] * frequency[None, :]
    return (jnp.cos(angles), jnp.sin(angles))


def rotate(values, cosine, sine):
    halfway = values.shape[-1] // 2
    leading = values[..., :halfway]
    trailing = values[..., halfway:]
    return jnp.concatenate(
        [leading * cosine - trailing * sine, trailing * cosine + leading * sine], axis=-1
    )


def unrotate(values, cosine, sine):
    halfway = values.shape[-1] // 2
    leading = values[..., :halfway]
    trailing = values[..., halfway:]
    return jnp.concatenate(
        [leading * cosine + trailing * sine, trailing * cosine - leading * sine], axis=-1
    )


def block_gradients(query_used, key_used, values, cotangent, first_row, length, prefix_rows):
    nope_dim = values.shape[-1]
    score_scale = query_used.shape[-1] ** (-0.5)
    scores = (
        jnp.einsum("qhd,khd->hqk", query_used, key_used, preferred_element_type=jnp.float32)
        * score_scale
    )
    row_index = first_row + jnp.arange(query_used.shape[0])
    col_index = jnp.arange(key_used.shape[0]) - prefix_rows
    allowed = (col_index[None, :] < 0) | (col_index[None, :] <= row_index[:, None]) & (
        col_index[None, :] < length
    )
    scores = jnp.where(allowed[None], scores, -jnp.inf)
    highest = jnp.max(scores, axis=-1, keepdims=True)
    exponent = jnp.exp(scores - highest)
    probability = exponent / jnp.sum(exponent, axis=-1, keepdims=True)
    weights = probability.astype(jnp.bfloat16)
    output = jnp.einsum("hqk,khv->qhv", weights, values, preferred_element_type=jnp.float32)
    row_delta = jnp.sum(cotangent.astype(jnp.float32) * output, axis=-1)
    prob_grad = jnp.einsum("qhv,khv->hqk", cotangent, values, preferred_element_type=jnp.float32)
    score_grad = (
        probability * (prob_grad - jnp.transpose(row_delta)[:, :, None]) * score_scale
    ).astype(jnp.bfloat16)
    query_part = jnp.einsum("hqk,khd->qhd", score_grad, key_used, preferred_element_type=jnp.float32)
    key_part = jnp.einsum("hqk,qhd->khd", score_grad, query_used, preferred_element_type=jnp.float32)
    nope_query = query_part[:, :, :nope_dim]
    rope_query = query_part[:, :, nope_dim:]
    nope_key = key_part[:, :, :nope_dim]
    rope_key = jnp.sum(key_part[:, :, nope_dim:], axis=1)
    value_grad = jnp.einsum("hqk,qhv->khv", weights, cotangent, preferred_element_type=jnp.float32)
    return (nope_query, rope_query, nope_key, rope_key, value_grad)


def swap_pair(values):
    return lax.ppermute(values, "core", [(0, 1), (1, 0)])


def on_device(queries, latent, prefix, kv_up, out_grad, lengths, positions):
    seq_len = queries.shape[0]
    latent_dim = kv_up.shape[0]
    value_dim = out_grad.shape[2]
    nope_dim = kv_up.shape[2] - value_dim
    rope_dim = latent.shape[1] - latent_dim
    prefix_rows = prefix.shape[0]
    length = lengths[0]
    cosine, sine = angles_of(positions[0], rope_dim)
    query_nope = queries[:, :, :nope_dim]
    query_rope = rotate(
        queries[:, :, nope_dim:].astype(jnp.float32), cosine[:, None], sine[:, None]
    ).astype(jnp.bfloat16)
    token_rope = rotate(latent[:, latent_dim:].astype(jnp.float32), cosine, sine).astype(
        jnp.bfloat16
    )
    source = jnp.concatenate(
        [prefix, jnp.concatenate([latent[:, :latent_dim], token_rope], axis=1)], axis=0
    )
    source_latent = source[:, :latent_dim]
    key_rope = source[:, latent_dim:]
    key_total = source.shape[0]
    live_rows = jnp.arange(seq_len) < length
    cotangent = jnp.where(live_rows[:, None, None], out_grad, jnp.zeros_like(out_grad))
    block_rows = min(seq_len, 128)
    head_part = kv_up.shape[1]
    projected = jnp.einsum(
        "kl,lhd->khd", source_latent, kv_up, preferred_element_type=jnp.float32
    ).astype(jnp.bfloat16)
    key_nope = projected[:, :, :nope_dim]
    values = projected[:, :, nope_dim:]
    query_used = jnp.concatenate([query_nope, query_rope], axis=-1)
    key_used = jnp.concatenate(
        [key_nope, jnp.broadcast_to(key_rope[:, None, :], key_rope.shape[:1] + (head_part,) + key_rope.shape[1:])],
        axis=-1,
    )
    nope_total = jnp.zeros((key_total, head_part, nope_dim), jnp.float32)
    rope_total = jnp.zeros((key_total, rope_dim), jnp.float32)
    value_total = jnp.zeros((key_total, head_part, value_dim), jnp.float32)
    query_pieces = []
    for block_number in range(seq_len // block_rows):
        first_row = block_number * block_rows
        last_row = first_row + block_rows
        seen = prefix_rows + last_row
        pieces = block_gradients(
            query_used[first_row:last_row],
            key_used[:seen],
            values[:seen],
            cotangent[first_row:last_row],
            first_row,
            length,
            prefix_rows,
        )
        nope_query, rope_query, nope_key, rope_key, value_grad = pieces
        nope_total = nope_total.at[:seen].add(nope_key)
        rope_total = rope_total.at[:seen].add(rope_key)
        value_total = value_total.at[:seen].add(value_grad)
        query_pieces.append(
            jnp.concatenate(
                [
                    nope_query,
                    unrotate(
                        rope_query, cosine[first_row:last_row, None], sine[first_row:last_row, None]
                    ),
                ],
                axis=-1,
            ).astype(jnp.bfloat16)
        )
    head_projected_grad = jnp.concatenate([nope_total, value_total], axis=-1).astype(jnp.bfloat16)
    up_part = jnp.einsum(
        "kl,khd->lhd", source_latent, head_projected_grad, preferred_element_type=jnp.float32
    )
    query_grad, projected_grad, rope_grad, up_part = (
        jnp.concatenate(query_pieces, axis=0),
        head_projected_grad,
        rope_total,
        up_part,
    )
    dp_size = lax.axis_size("dp")
    up_pieces = lax.all_to_all(
        up_part.astype(jnp.bfloat16).reshape((dp_size, -1) + up_part.shape[1:]), "dp", 0, 0, tiled=False
    )
    up_grad = jnp.sum(up_pieces.astype(jnp.float32), axis=0)
    token_grad = projected_grad[prefix_rows:]
    token_rope_grad = rope_grad[prefix_rows:]
    latent_part = jnp.einsum("khd,lhd->kl", token_grad, kv_up, preferred_element_type=jnp.float32)
    token_part = jnp.concatenate(
        [latent_part, unrotate(token_rope_grad, cosine, sine)], axis=1
    ).astype(jnp.bfloat16)
    core = lax.axis_index("core")
    pair_size = lax.axis_size("core")
    row_size = lax.axis_size("hr")
    token_blocks = token_part.reshape((row_size, pair_size, -1) + token_part.shape[1:])
    token_mine = jnp.where(core == 0, token_blocks[:, 0], token_blocks[:, 1])
    token_other = jnp.where(core == 0, token_blocks[:, 1], token_blocks[:, 0])
    token_pair = (
        token_mine.astype(jnp.float32) + swap_pair(token_other).astype(jnp.float32)
    ).astype(jnp.bfloat16)
    token_pieces = lax.all_to_all(token_pair, "hr", 0, 0, tiled=False)
    latent_grad = jnp.sum(token_pieces.astype(jnp.float32), axis=0)
    latent_part = jnp.einsum(
        "khd,lhd->kl", projected_grad[:prefix_rows], kv_up, preferred_element_type=jnp.float32
    )
    prefix_part = jnp.concatenate([latent_part, rope_grad[:prefix_rows]], axis=1)
    half_rows = prefix_part.shape[0] // 2
    prefix_mine = lax.dynamic_slice_in_dim(prefix_part, core * half_rows, half_rows)
    prefix_other = lax.dynamic_slice_in_dim(prefix_part, (1 - core) * half_rows, half_rows)
    prefix_half = prefix_mine + swap_pair(prefix_other)
    prefix_rows_part = jnp.sum(
        lax.all_to_all(
            prefix_half.reshape((row_size, -1) + prefix_half.shape[1:]), "hr", 0, 0, tiled=False
        ),
        axis=0,
    )
    prefix_own = prefix_rows_part
    stride = 1
    while stride < dp_size:
        partners = [(i, i ^ stride) for i in range(dp_size)]
        prefix_own = prefix_own + lax.ppermute(prefix_own, "dp", partners)
        stride *= 2
    prefix_copies = jnp.broadcast_to(prefix_own[None], (row_size,) + prefix_own.shape)
    prefix_gathered = lax.all_to_all(prefix_copies, "hr", 0, 0, tiled=False).reshape(
        prefix_half.shape
    )
    prefix_partner = swap_pair(prefix_gathered)
    prefix_grad = jnp.where(
        core == 0,
        jnp.concatenate([prefix_gathered, prefix_partner], axis=0),
        jnp.concatenate([prefix_partner, prefix_gathered], axis=0),
    )
    return (query_grad, latent_grad, up_grad, prefix_grad)


def solution(mesh):
    dp_size, head_size = mesh.shape["dp"], mesh.shape["head"]
    split = Mesh(mesh.devices.reshape(dp_size, head_size // 2, 2), ("dp", "hr", "core"))
    head = ("hr", "core")
    placed = (
        P("dp", head, None),
        P("dp", None),
        P(),
        P(None, head, None),
        P("dp", head, None),
        P("dp"),
        P("dp", None),
    )
    return jax.shard_map(
        on_device,
        mesh=split,
        in_specs=placed,
        out_specs=(P("dp", head, None), P(("dp",) + head, None), P("dp", head, None), P()),
        check_vma=False,
    )
```

```python
import jax
import jax.numpy as jnp
from jax import lax
from jax.sharding import Mesh, PartitionSpec as P


def angles_of(positions, rope_dim):
    halfway = rope_dim // 2
    frequency = 10000.0 ** (-(jnp.arange(halfway, dtype=jnp.float32) * 2.0 / rope_dim))
    angles = positions.astype(jnp.float32)[:, None] * frequency[None, :]
    return (jnp.cos(angles), jnp.sin(angles))


def rotate(values, cosine, sine):
    halfway = values.shape[-1] // 2
    leading = values[..., :halfway]
    trailing = values[..., halfway:]
    return jnp.concatenate(
        [leading * cosine - trailing * sine, trailing * cosine + leading * sine], axis=-1
    )


def unrotate(values, cosine, sine):
    halfway = values.shape[-1] // 2
    leading = values[..., :halfway]
    trailing = values[..., halfway:]
    return jnp.concatenate(
        [leading * cosine + trailing * sine, trailing * cosine - leading * sine], axis=-1
    )


def block_gradients(query_used, key_used, values, cotangent, first_row, length, prefix_rows):
    nope_dim = values.shape[-1]
    score_scale = query_used.shape[-1] ** (-0.5)
    scores = (
        jnp.einsum("qhd,khd->hqk", query_used, key_used, preferred_element_type=jnp.float32)
        * score_scale
    )
    row_index = first_row + jnp.arange(query_used.shape[0])
    col_index = jnp.arange(key_used.shape[0]) - prefix_rows
    allowed = (col_index[None, :] < 0) | (col_index[None, :] <= row_index[:, None]) & (
        col_index[None, :] < length
    )
    scores = jnp.where(allowed[None], scores, -jnp.inf)
    highest = jnp.max(scores, axis=-1, keepdims=True)
    exponent = jnp.exp(scores - highest)
    probability = exponent / jnp.sum(exponent, axis=-1, keepdims=True)
    weights = probability.astype(jnp.bfloat16)
    output = jnp.einsum("hqk,khv->qhv", weights, values, preferred_element_type=jnp.float32)
    row_delta = jnp.sum(cotangent.astype(jnp.float32) * output, axis=-1)
    prob_grad = jnp.einsum("qhv,khv->hqk", cotangent, values, preferred_element_type=jnp.float32)
    score_grad = (
        probability * (prob_grad - jnp.transpose(row_delta)[:, :, None]) * score_scale
    ).astype(jnp.bfloat16)
    query_part = jnp.einsum("hqk,khd->qhd", score_grad, key_used, preferred_element_type=jnp.float32)
    key_part = jnp.einsum("hqk,qhd->khd", score_grad, query_used, preferred_element_type=jnp.float32)
    nope_query = query_part[:, :, :nope_dim]
    rope_query = query_part[:, :, nope_dim:]
    nope_key = key_part[:, :, :nope_dim]
    rope_key = jnp.sum(key_part[:, :, nope_dim:], axis=1)
    value_grad = jnp.einsum("hqk,qhv->khv", weights, cotangent, preferred_element_type=jnp.float32)
    return (nope_query, rope_query, nope_key, rope_key, value_grad)


def swap_pair(values):
    return lax.ppermute(values, "core", [(0, 1), (1, 0)])


def on_device(queries, latent, prefix, kv_up, out_grad, lengths, positions):
    seq_len = queries.shape[0]
    latent_dim = kv_up.shape[0]
    value_dim = out_grad.shape[2]
    nope_dim = kv_up.shape[2] - value_dim
    rope_dim = latent.shape[1] - latent_dim
    prefix_rows = prefix.shape[0]
    length = lengths[0]
    cosine, sine = angles_of(positions[0], rope_dim)
    query_nope = queries[:, :, :nope_dim]
    query_rope = rotate(
        queries[:, :, nope_dim:].astype(jnp.float32), cosine[:, None], sine[:, None]
    ).astype(jnp.bfloat16)
    token_rope = rotate(latent[:, latent_dim:].astype(jnp.float32), cosine, sine).astype(
        jnp.bfloat16
    )
    source = jnp.concatenate(
        [prefix, jnp.concatenate([latent[:, :latent_dim], token_rope], axis=1)], axis=0
    )
    source_latent = source[:, :latent_dim]
    key_rope = source[:, latent_dim:]
    key_total = source.shape[0]
    live_rows = jnp.arange(seq_len) < length
    cotangent = jnp.where(live_rows[:, None, None], out_grad, jnp.zeros_like(out_grad))
    block_rows = min(seq_len, 256)
    head_part = kv_up.shape[1]
    projected = jnp.einsum(
        "kl,lhd->khd", source_latent, kv_up, preferred_element_type=jnp.float32
    ).astype(jnp.bfloat16)
    key_nope = projected[:, :, :nope_dim]
    values = projected[:, :, nope_dim:]
    query_used = jnp.concatenate([query_nope, query_rope], axis=-1)
    key_used = jnp.concatenate(
        [key_nope, jnp.broadcast_to(key_rope[:, None, :], key_rope.shape[:1] + (head_part,) + key_rope.shape[1:])],
        axis=-1,
    )
    nope_total = jnp.zeros((key_total, head_part, nope_dim), jnp.float32)
    rope_total = jnp.zeros((key_total, rope_dim), jnp.float32)
    value_total = jnp.zeros((key_total, head_part, value_dim), jnp.float32)
    query_pieces = []
    bounds = (0, seq_len // 2, 3 * seq_len // 4, seq_len)
    for first_row, last_row in zip(bounds[:-1], bounds[1:]):
        seen = prefix_rows + last_row
        pieces = block_gradients(
            query_used[first_row:last_row],
            key_used[:seen],
            values[:seen],
            cotangent[first_row:last_row],
            first_row,
            length,
            prefix_rows,
        )
        nope_query, rope_query, nope_key, rope_key, value_grad = pieces
        nope_total = nope_total.at[:seen].add(nope_key)
        rope_total = rope_total.at[:seen].add(rope_key)
        value_total = value_total.at[:seen].add(value_grad)
        query_pieces.append(
            jnp.concatenate(
                [
                    nope_query,
                    unrotate(
                        rope_query, cosine[first_row:last_row, None], sine[first_row:last_row, None]
                    ),
                ],
                axis=-1,
            ).astype(jnp.bfloat16)
        )
    head_projected_grad = jnp.concatenate([nope_total, value_total], axis=-1).astype(jnp.bfloat16)
    up_part = jnp.einsum(
        "kl,khd->lhd", source_latent, head_projected_grad, preferred_element_type=jnp.float32
    )
    query_grad, projected_grad, rope_grad, up_part = (
        jnp.concatenate(query_pieces, axis=0),
        head_projected_grad,
        rope_total,
        up_part,
    )
    dp_size = lax.axis_size("dp")
    up_pieces = lax.all_to_all(
        up_part.astype(jnp.bfloat16).reshape((dp_size, -1) + up_part.shape[1:]), "dp", 0, 0, tiled=False
    )
    up_grad = jnp.sum(up_pieces.astype(jnp.float32), axis=0)
    token_grad = projected_grad[prefix_rows:]
    token_rope_grad = rope_grad[prefix_rows:]
    latent_part = jnp.einsum("khd,lhd->kl", token_grad, kv_up, preferred_element_type=jnp.float32)
    token_part = jnp.concatenate(
        [latent_part, unrotate(token_rope_grad, cosine, sine)], axis=1
    ).astype(jnp.bfloat16)
    core = lax.axis_index("core")
    pair_size = lax.axis_size("core")
    row_size = lax.axis_size("hr")
    token_blocks = token_part.reshape((row_size, pair_size, -1) + token_part.shape[1:])
    token_mine = jnp.where(core == 0, token_blocks[:, 0], token_blocks[:, 1])
    token_other = jnp.where(core == 0, token_blocks[:, 1], token_blocks[:, 0])
    token_pair = (
        token_mine.astype(jnp.float32) + swap_pair(token_other).astype(jnp.float32)
    ).astype(jnp.bfloat16)
    token_pieces = lax.all_to_all(token_pair, "hr", 0, 0, tiled=False)
    latent_grad = jnp.sum(token_pieces.astype(jnp.float32), axis=0)
    latent_part = jnp.einsum(
        "khd,lhd->kl", projected_grad[:prefix_rows], kv_up, preferred_element_type=jnp.float32
    )
    prefix_part = jnp.concatenate([latent_part, rope_grad[:prefix_rows]], axis=1)
    half_rows = prefix_part.shape[0] // 2
    prefix_mine = lax.dynamic_slice_in_dim(prefix_part, core * half_rows, half_rows)
    prefix_other = lax.dynamic_slice_in_dim(prefix_part, (1 - core) * half_rows, half_rows)
    prefix_half = prefix_mine + swap_pair(prefix_other)
    prefix_rows_part = jnp.sum(
        lax.all_to_all(
            prefix_half.reshape((row_size, -1) + prefix_half.shape[1:]), "hr", 0, 0, tiled=False
        ),
        axis=0,
    )
    prefix_own = prefix_rows_part
    stride = 1
    while stride < dp_size:
        partners = [(i, i ^ stride) for i in range(dp_size)]
        prefix_own = prefix_own + lax.ppermute(prefix_own, "dp", partners)
        stride *= 2
    prefix_copies = jnp.broadcast_to(prefix_own[None], (row_size,) + prefix_own.shape)
    prefix_gathered = lax.all_to_all(prefix_copies, "hr", 0, 0, tiled=False).reshape(
        prefix_half.shape
    )
    prefix_partner = swap_pair(prefix_gathered)
    prefix_grad = jnp.where(
        core == 0,
        jnp.concatenate([prefix_gathered, prefix_partner], axis=0),
        jnp.concatenate([prefix_partner, prefix_gathered], axis=0),
    )
    return (query_grad, latent_grad, up_grad, prefix_grad)


def solution(mesh):
    dp_size, head_size = mesh.shape["dp"], mesh.shape["head"]
    split = Mesh(mesh.devices.reshape(dp_size, head_size // 2, 2), ("dp", "hr", "core"))
    head = ("hr", "core")
    placed = (
        P("dp", head, None),
        P("dp", None),
        P(),
        P(None, head, None),
        P("dp", head, None),
        P("dp"),
        P("dp", None),
    )
    return jax.shard_map(
        on_device,
        mesh=split,
        in_specs=placed,
        out_specs=(P("dp", head, None), P(("dp",) + head, None), P("dp", head, None), P()),
        check_vma=False,
    )
```

```python
import jax
import jax.numpy as jnp
from jax import lax
from jax.sharding import Mesh, PartitionSpec as P


def angles_of(positions, rope_dim):
    halfway = rope_dim // 2
    frequency = 10000.0 ** (-(jnp.arange(halfway, dtype=jnp.float32) * 2.0 / rope_dim))
    angles = positions.astype(jnp.float32)[:, None] * frequency[None, :]
    return (jnp.cos(angles), jnp.sin(angles))


def rotate(values, cosine, sine):
    halfway = values.shape[-1] // 2
    leading = values[..., :halfway]
    trailing = values[..., halfway:]
    return jnp.concatenate(
        [leading * cosine - trailing * sine, trailing * cosine + leading * sine], axis=-1
    )


def unrotate(values, cosine, sine):
    halfway = values.shape[-1] // 2
    leading = values[..., :halfway]
    trailing = values[..., halfway:]
    return jnp.concatenate(
        [leading * cosine + trailing * sine, trailing * cosine - leading * sine], axis=-1
    )


def block_gradients(query_used, key_used, values, cotangent, first_row, length, prefix_rows):
    nope_dim = values.shape[-1]
    score_scale = query_used.shape[-1] ** (-0.5)
    scores = (
        jnp.einsum("qhd,khd->hqk", query_used, key_used, preferred_element_type=jnp.float32)
        * score_scale
    )
    row_index = first_row + jnp.arange(query_used.shape[0])
    col_index = jnp.arange(key_used.shape[0]) - prefix_rows
    allowed = (col_index[None, :] < 0) | (col_index[None, :] <= row_index[:, None]) & (
        col_index[None, :] < length
    )
    scores = jnp.where(allowed[None], scores, -jnp.inf)
    highest = jnp.max(scores, axis=-1, keepdims=True)
    exponent = jnp.exp(scores - highest)
    probability = exponent / jnp.sum(exponent, axis=-1, keepdims=True)
    weights = probability.astype(jnp.bfloat16)
    prob_grad = jnp.einsum("qhv,khv->hqk", cotangent, values, preferred_element_type=jnp.float32)
    row_delta = jnp.sum(weights.astype(jnp.float32) * prob_grad, axis=-1, keepdims=True)
    score_grad = (probability * (prob_grad - row_delta) * score_scale).astype(jnp.bfloat16)
    query_part = jnp.einsum("hqk,khd->qhd", score_grad, key_used, preferred_element_type=jnp.float32)
    key_part = jnp.einsum("hqk,qhd->khd", score_grad, query_used, preferred_element_type=jnp.float32)
    nope_query = query_part[:, :, :nope_dim]
    rope_query = query_part[:, :, nope_dim:]
    nope_key = key_part[:, :, :nope_dim]
    rope_key = jnp.sum(key_part[:, :, nope_dim:], axis=1)
    value_grad = jnp.einsum("hqk,qhv->khv", weights, cotangent, preferred_element_type=jnp.float32)
    return (nope_query, rope_query, nope_key, rope_key, value_grad)


def swap_pair(values):
    return lax.ppermute(values, "core", [(0, 1), (1, 0)])


def on_device(queries, latent, prefix, kv_up, out_grad, lengths, positions):
    seq_len = queries.shape[0]
    latent_dim = kv_up.shape[0]
    value_dim = out_grad.shape[2]
    nope_dim = kv_up.shape[2] - value_dim
    rope_dim = latent.shape[1] - latent_dim
    prefix_rows = prefix.shape[0]
    length = lengths[0]
    cosine, sine = angles_of(positions[0], rope_dim)
    query_nope = queries[:, :, :nope_dim]
    query_rope = rotate(
        queries[:, :, nope_dim:].astype(jnp.float32), cosine[:, None], sine[:, None]
    ).astype(jnp.bfloat16)
    token_rope = rotate(latent[:, latent_dim:].astype(jnp.float32), cosine, sine).astype(
        jnp.bfloat16
    )
    source = jnp.concatenate(
        [prefix, jnp.concatenate([latent[:, :latent_dim], token_rope], axis=1)], axis=0
    )
    source_latent = source[:, :latent_dim]
    key_rope = source[:, latent_dim:]
    key_total = source.shape[0]
    live_rows = jnp.arange(seq_len) < length
    cotangent = jnp.where(live_rows[:, None, None], out_grad, jnp.zeros_like(out_grad))
    block_rows = min(seq_len, 256)
    head_part = kv_up.shape[1]
    projected = jnp.einsum(
        "kl,lhd->khd", source_latent, kv_up, preferred_element_type=jnp.float32
    ).astype(jnp.bfloat16)
    key_nope = projected[:, :, :nope_dim]
    values = projected[:, :, nope_dim:]
    query_used = jnp.concatenate([query_nope, query_rope], axis=-1)
    key_used = jnp.concatenate(
        [key_nope, jnp.broadcast_to(key_rope[:, None, :], key_rope.shape[:1] + (head_part,) + key_rope.shape[1:])],
        axis=-1,
    )
    nope_total = jnp.zeros((key_total, head_part, nope_dim), jnp.float32)
    rope_total = jnp.zeros((key_total, rope_dim), jnp.float32)
    value_total = jnp.zeros((key_total, head_part, value_dim), jnp.float32)
    query_pieces = []
    for block_number in range(seq_len // block_rows):
        first_row = block_number * block_rows
        last_row = first_row + block_rows
        seen = prefix_rows + last_row
        pieces = block_gradients(
            query_used[first_row:last_row],
            key_used[:seen],
            values[:seen],
            cotangent[first_row:last_row],
            first_row,
            length,
            prefix_rows,
        )
        nope_query, rope_query, nope_key, rope_key, value_grad = pieces
        nope_total = nope_total.at[:seen].add(nope_key)
        rope_total = rope_total.at[:seen].add(rope_key)
        value_total = value_total.at[:seen].add(value_grad)
        query_pieces.append(
            jnp.concatenate(
                [
                    nope_query,
                    unrotate(
                        rope_query, cosine[first_row:last_row, None], sine[first_row:last_row, None]
                    ),
                ],
                axis=-1,
            ).astype(jnp.bfloat16)
        )
    head_projected_grad = jnp.concatenate([nope_total, value_total], axis=-1).astype(jnp.bfloat16)
    up_part = jnp.einsum(
        "kl,khd->lhd", source_latent, head_projected_grad, preferred_element_type=jnp.float32
    )
    query_grad, projected_grad, rope_grad, up_part = (
        jnp.concatenate(query_pieces, axis=0),
        head_projected_grad,
        rope_total,
        up_part,
    )
    dp_size = lax.axis_size("dp")
    up_pieces = lax.all_to_all(
        up_part.astype(jnp.bfloat16).reshape((dp_size, -1) + up_part.shape[1:]), "dp", 0, 0, tiled=False
    )
    up_grad = jnp.sum(up_pieces.astype(jnp.float32), axis=0)
    token_grad = projected_grad[prefix_rows:]
    token_rope_grad = rope_grad[prefix_rows:]
    latent_part = jnp.einsum("khd,lhd->kl", token_grad, kv_up, preferred_element_type=jnp.float32)
    token_part = jnp.concatenate(
        [latent_part, unrotate(token_rope_grad, cosine, sine)], axis=1
    ).astype(jnp.bfloat16)
    core = lax.axis_index("core")
    pair_size = lax.axis_size("core")
    row_size = lax.axis_size("hr")
    token_blocks = token_part.reshape((row_size, pair_size, -1) + token_part.shape[1:])
    token_mine = jnp.where(core == 0, token_blocks[:, 0], token_blocks[:, 1])
    token_other = jnp.where(core == 0, token_blocks[:, 1], token_blocks[:, 0])
    token_pair = (
        token_mine.astype(jnp.float32) + swap_pair(token_other).astype(jnp.float32)
    ).astype(jnp.bfloat16)
    token_pieces = lax.all_to_all(token_pair, "hr", 0, 0, tiled=False)
    latent_grad = jnp.sum(token_pieces.astype(jnp.float32), axis=0)
    latent_part = jnp.einsum(
        "khd,lhd->kl", projected_grad[:prefix_rows], kv_up, preferred_element_type=jnp.float32
    )
    prefix_part = jnp.concatenate([latent_part, rope_grad[:prefix_rows]], axis=1)
    half_rows = prefix_part.shape[0] // 2
    prefix_mine = lax.dynamic_slice_in_dim(prefix_part, core * half_rows, half_rows)
    prefix_other = lax.dynamic_slice_in_dim(prefix_part, (1 - core) * half_rows, half_rows)
    prefix_half = prefix_mine + swap_pair(prefix_other)
    prefix_rows_part = jnp.sum(
        lax.all_to_all(
            prefix_half.reshape((row_size, -1) + prefix_half.shape[1:]), "hr", 0, 0, tiled=False
        ),
        axis=0,
    )
    prefix_own = prefix_rows_part
    stride = 1
    while stride < dp_size:
        partners = [(i, i ^ stride) for i in range(dp_size)]
        prefix_own = prefix_own + lax.ppermute(prefix_own, "dp", partners)
        stride *= 2
    prefix_copies = jnp.broadcast_to(prefix_own[None], (row_size,) + prefix_own.shape)
    prefix_gathered = lax.all_to_all(prefix_copies, "hr", 0, 0, tiled=False).reshape(
        prefix_half.shape
    )
    prefix_partner = swap_pair(prefix_gathered)
    prefix_grad = jnp.where(
        core == 0,
        jnp.concatenate([prefix_gathered, prefix_partner], axis=0),
        jnp.concatenate([prefix_partner, prefix_gathered], axis=0),
    )
    return (query_grad, latent_grad, up_grad, prefix_grad)


def solution(mesh):
    dp_size, head_size = mesh.shape["dp"], mesh.shape["head"]
    split = Mesh(mesh.devices.reshape(dp_size, head_size // 2, 2), ("dp", "hr", "core"))
    head = ("hr", "core")
    placed = (
        P("dp", head, None),
        P("dp", None),
        P(),
        P(None, head, None),
        P("dp", head, None),
        P("dp"),
        P("dp", None),
    )
    return jax.shard_map(
        on_device,
        mesh=split,
        in_specs=placed,
        out_specs=(P("dp", head, None), P(("dp",) + head, None), P("dp", head, None), P()),
        check_vma=False,
    )
```

```python
import jax
import jax.numpy as jnp
from jax import lax
from jax.sharding import Mesh, PartitionSpec as P


def angles_of(positions, rope_dim):
    halfway = rope_dim // 2
    frequency = 10000.0 ** (-(jnp.arange(halfway, dtype=jnp.float32) * 2.0 / rope_dim))
    angles = positions.astype(jnp.float32)[:, None] * frequency[None, :]
    return (jnp.cos(angles), jnp.sin(angles))


def rotate(values, cosine, sine):
    halfway = values.shape[-1] // 2
    leading = values[..., :halfway]
    trailing = values[..., halfway:]
    return jnp.concatenate(
        [leading * cosine - trailing * sine, trailing * cosine + leading * sine], axis=-1
    )


def unrotate(values, cosine, sine):
    halfway = values.shape[-1] // 2
    leading = values[..., :halfway]
    trailing = values[..., halfway:]
    return jnp.concatenate(
        [leading * cosine + trailing * sine, trailing * cosine - leading * sine], axis=-1
    )


def block_gradients(query_used, key_used, values, cotangent, first_row, length, prefix_rows):
    nope_dim = values.shape[-1]
    score_scale = query_used.shape[-1] ** (-0.5)
    scores = (
        jnp.einsum("qhd,khd->hqk", query_used, key_used, preferred_element_type=jnp.float32)
        * score_scale
    )
    row_index = first_row + jnp.arange(query_used.shape[0])
    col_index = jnp.arange(key_used.shape[0]) - prefix_rows
    allowed = (col_index[None, :] < 0) | (col_index[None, :] <= row_index[:, None]) & (
        col_index[None, :] < length
    )
    scores = jnp.where(allowed[None], scores, -jnp.inf)
    highest = jnp.max(scores, axis=-1, keepdims=True)
    exponent = jnp.exp(scores - highest)
    probability = exponent / jnp.sum(exponent, axis=-1, keepdims=True)
    weights = probability.astype(jnp.bfloat16)
    output = jnp.einsum("hqk,khv->qhv", weights, values, preferred_element_type=jnp.float32)
    row_delta = jnp.sum(cotangent.astype(jnp.float32) * output, axis=-1)
    prob_grad = jnp.einsum("qhv,khv->hqk", cotangent, values, preferred_element_type=jnp.float32)
    score_grad = (
        probability * (prob_grad - jnp.transpose(row_delta)[:, :, None]) * score_scale
    ).astype(jnp.bfloat16)
    query_part = jnp.einsum("hqk,khd->qhd", score_grad, key_used, preferred_element_type=jnp.float32)
    key_part = jnp.einsum("hqk,qhd->khd", score_grad, query_used, preferred_element_type=jnp.float32)
    nope_query = query_part[:, :, :nope_dim]
    rope_query = query_part[:, :, nope_dim:]
    nope_key = key_part[:, :, :nope_dim]
    rope_key = jnp.sum(key_part[:, :, nope_dim:], axis=1)
    value_grad = jnp.einsum("hqk,qhv->khv", weights, cotangent, preferred_element_type=jnp.float32)
    return (nope_query, rope_query, nope_key, rope_key, value_grad)


def swap_pair(values):
    return lax.ppermute(values, "core", [(0, 1), (1, 0)])


def on_device(queries, latent, prefix, kv_up, out_grad, lengths, positions):
    seq_len = queries.shape[0]
    latent_dim = kv_up.shape[0]
    value_dim = out_grad.shape[2]
    nope_dim = kv_up.shape[2] - value_dim
    rope_dim = latent.shape[1] - latent_dim
    prefix_rows = prefix.shape[0]
    length = lengths[0]
    cosine, sine = angles_of(positions[0], rope_dim)
    query_nope = queries[:, :, :nope_dim]
    query_rope = rotate(
        queries[:, :, nope_dim:].astype(jnp.float32), cosine[:, None], sine[:, None]
    ).astype(jnp.bfloat16)
    token_rope = rotate(latent[:, latent_dim:].astype(jnp.float32), cosine, sine).astype(
        jnp.bfloat16
    )
    source = jnp.concatenate(
        [prefix, jnp.concatenate([latent[:, :latent_dim], token_rope], axis=1)], axis=0
    )
    source_latent = source[:, :latent_dim]
    key_rope = source[:, latent_dim:]
    key_total = source.shape[0]
    live_rows = jnp.arange(seq_len) < length
    cotangent = jnp.where(live_rows[:, None, None], out_grad, jnp.zeros_like(out_grad))
    block_rows = min(seq_len, 256)
    head_part = kv_up.shape[1]
    projected = jnp.einsum(
        "kl,lhd->khd", source_latent, kv_up, preferred_element_type=jnp.float32
    ).astype(jnp.bfloat16)
    key_nope = projected[:, :, :nope_dim]
    values = projected[:, :, nope_dim:]
    query_used = jnp.concatenate([query_nope, query_rope], axis=-1)
    key_used = jnp.concatenate(
        [key_nope, jnp.broadcast_to(key_rope[:, None, :], key_rope.shape[:1] + (head_part,) + key_rope.shape[1:])],
        axis=-1,
    )
    nope_total = jnp.zeros((key_total, head_part, nope_dim), jnp.float32)
    rope_total = jnp.zeros((key_total, rope_dim), jnp.float32)
    value_total = jnp.zeros((key_total, head_part, value_dim), jnp.float32)
    query_pieces = []
    for block_number in range(seq_len // block_rows):
        first_row = block_number * block_rows
        last_row = first_row + block_rows
        seen = prefix_rows + last_row
        pieces = block_gradients(
            query_used[first_row:last_row],
            key_used[:seen],
            values[:seen],
            cotangent[first_row:last_row],
            first_row,
            length,
            prefix_rows,
        )
        nope_query, rope_query, nope_key, rope_key, value_grad = pieces
        nope_total = nope_total.at[:seen].add(nope_key)
        rope_total = rope_total.at[:seen].add(rope_key)
        value_total = value_total.at[:seen].add(value_grad)
        query_pieces.append(
            jnp.concatenate(
                [
                    nope_query,
                    unrotate(
                        rope_query, cosine[first_row:last_row, None], sine[first_row:last_row, None]
                    ),
                ],
                axis=-1,
            ).astype(jnp.bfloat16)
        )
    head_projected_grad = jnp.concatenate([nope_total, value_total], axis=-1).astype(jnp.bfloat16)
    up_part = jnp.einsum(
        "kl,khd->lhd", source_latent, head_projected_grad, preferred_element_type=jnp.float32
    )
    query_grad, projected_grad, rope_grad, up_part = (
        jnp.concatenate(query_pieces, axis=0),
        head_projected_grad,
        rope_total,
        up_part,
    )
    dp_size = lax.axis_size("dp")
    up_pieces = lax.all_to_all(
        up_part.astype(jnp.bfloat16).reshape((dp_size, -1) + up_part.shape[1:]), "dp", 0, 0, tiled=False
    )
    up_grad = jnp.sum(up_pieces.astype(jnp.float32), axis=0)
    token_grad = projected_grad[prefix_rows:]
    token_rope_grad = rope_grad[prefix_rows:]
    latent_part = jnp.einsum("khd,lhd->kl", token_grad, kv_up, preferred_element_type=jnp.float32)
    token_part = jnp.concatenate(
        [latent_part, unrotate(token_rope_grad, cosine, sine)], axis=1
    ).astype(jnp.bfloat16)
    core = lax.axis_index("core")
    pair_size = lax.axis_size("core")
    row_size = lax.axis_size("hr")
    token_blocks = token_part.reshape((row_size, pair_size, -1) + token_part.shape[1:])
    token_mine = jnp.where(core == 0, token_blocks[:, 0], token_blocks[:, 1])
    token_other = jnp.where(core == 0, token_blocks[:, 1], token_blocks[:, 0])
    token_pair = (
        token_mine.astype(jnp.float32) + swap_pair(token_other).astype(jnp.float32)
    ).astype(jnp.bfloat16)
    token_pieces = lax.all_to_all(token_pair, "hr", 0, 0, tiled=False)
    latent_grad = jnp.sum(token_pieces.astype(jnp.float32), axis=0)
    latent_part = jnp.einsum(
        "khd,lhd->kl", projected_grad[:prefix_rows], kv_up, preferred_element_type=jnp.float32
    )
    prefix_part = jnp.concatenate([latent_part, rope_grad[:prefix_rows]], axis=1)
    half_rows = prefix_part.shape[0] // 2
    prefix_mine = lax.dynamic_slice_in_dim(prefix_part, core * half_rows, half_rows)
    prefix_other = lax.dynamic_slice_in_dim(prefix_part, (1 - core) * half_rows, half_rows)
    prefix_half = prefix_mine + swap_pair(prefix_other)
    prefix_rows_part = jnp.sum(
        lax.all_to_all(
            prefix_half.reshape((row_size, -1) + prefix_half.shape[1:]), "hr", 0, 0, tiled=False
        ),
        axis=0,
    )
    prefix_own = prefix_rows_part
    stride = 1
    while stride < dp_size:
        partners = [(i, i ^ stride) for i in range(dp_size)]
        prefix_own = prefix_own + lax.ppermute(prefix_own, "dp", partners)
        stride *= 2
    prefix_sent = prefix_own.astype(jnp.bfloat16)
    prefix_copies = jnp.broadcast_to(prefix_sent[None], (row_size,) + prefix_sent.shape)
    prefix_gathered = lax.all_to_all(prefix_copies, "hr", 0, 0, tiled=False).reshape(
        prefix_half.shape
    )
    prefix_partner = swap_pair(prefix_gathered)
    prefix_grad = jnp.where(
        core == 0,
        jnp.concatenate([prefix_gathered, prefix_partner], axis=0),
        jnp.concatenate([prefix_partner, prefix_gathered], axis=0),
    ).astype(jnp.float32)
    return (query_grad, latent_grad, up_grad, prefix_grad)


def solution(mesh):
    dp_size, head_size = mesh.shape["dp"], mesh.shape["head"]
    split = Mesh(mesh.devices.reshape(dp_size, head_size // 2, 2), ("dp", "hr", "core"))
    head = ("hr", "core")
    placed = (
        P("dp", head, None),
        P("dp", None),
        P(),
        P(None, head, None),
        P("dp", head, None),
        P("dp"),
        P("dp", None),
    )
    return jax.shard_map(
        on_device,
        mesh=split,
        in_specs=placed,
        out_specs=(P("dp", head, None), P(("dp",) + head, None), P("dp", head, None), P()),
        check_vma=False,
    )
```
